32 devices in a mesh: clips: 2 (over y), rows: 4 (over z), tm: 2 (over x), chan: 2 (over core).
Axes of the slice: x: 2, y: 2, z: 4, core: 2. Of those that a mesh axis runs over, the one named last changes fastest.
Arguments:
- latent: bfloat16 [8, 4, 64, 512], P(('clips', 'tm'), 'rows', None, 'chan'), parts along dimension 0, may hold values from -24 to 24, as said below
- norm1_gain: float32 [512], P('chan'), may hold values from 0.5 to 1.5
- norm1_bias: float32 [512], P('chan'), may hold values from -1.2 to 1.2
- conv_weight: bfloat16 [13824, 512], P('rows', 'chan'), may hold values from -0.0546875 to 0.0546875
- conv_bias: float32 [512], P('chan'), may hold values from -1.2 to 1.2
- norm2_gain: float32 [512], P('chan'), may hold values from 0.5 to 1.5
- norm2_bias: float32 [512], P('chan'), may hold values from -1.2 to 1.2
- w_query: bfloat16 [512, 512], replicated, may hold values from -2 to 2
- b_query: float32 [512], replicated, may hold values from -1.2 to 1.2
- w_key: bfloat16 [512, 512], replicated, may hold values from -3 to 3
- w_value: bfloat16 [512, 512], replicated, may hold values from -0.25 to 0.25
- b_value: float32 [512], replicated, may hold values from -1.2 to 1.2
- w_out: bfloat16 [512, 512], replicated, may hold values from -0.25 to 0.25
- b_out: float32 [512], replicated, may hold values from -1.2 to 1.2
Outputs:
- decoded: bfloat16 [8, 4, 64, 512], P(('clips', 'tm'), 'rows', None, 'chan'), parts along dimension 0
The draws below stay inside these ranges and needn't reach their ends.
There are 2 independent parts, one for each index of `clips`. The reference program is written for one: setup_inputs(seed, part) draws one part's arguments, and reference() takes and returns one part's arrays. A program takes and returns all parts, laid end to end along the dimension named above; an argument that names none is the same for every part. Nothing has to cross between parts.
Inputs may be any that keep to these rules, and one draw needn't show every extreme that they name: `latent`: activations of order one.
All inputs are finite; a program needn't handle non-finite values.
Results may differ from the reference program's by a relative error of at most 0.012.
The reference program's roundings to bfloat16 on the way count: a program that leaves them out, or rounds other values in their place, can miss the bound.
Values may be sent and summed in bfloat16 or wider, within the bound.
No kernel may reach another device: no remote copies, remote signals or barrier semaphores. Data moves between devices by JAX's collectives and lax.ppermute only.
A program may use at most 64 MiB of HBM per device.

```python
import math
import jax
import jax.numpy as jnp
from jax import lax

C = 512
GROUPS = 32
TAPS = 27
W = 64
FRAMES = 4
H = 4


def draw_latent(key, part):
    noise_key, spread_key = jax.random.split(key)
    row_frac = jnp.arange(H, dtype=jnp.float32) / (H - 1)
    ramp_rows = (1.0 + 2.0 * row_frac)[None, :, None, None]
    sample = jnp.clip(jax.random.normal(noise_key, (FRAMES, H, W, C), jnp.float32), -4.0, 4.0)
    spread = jnp.exp(jax.random.uniform(spread_key, (FRAMES, H, W, 1), jnp.float32, math.log(0.2), math.log(2.0)))
    return (sample * spread * ramp_rows).astype(jnp.bfloat16)


def query_key_pair(key):
    fold_query = jax.random.fold_in(key, 101)
    fold_key = jax.random.fold_in(key, 202)
    scale_size = 1.75 / math.sqrt(C)
    extra_noise = jnp.clip(jax.random.normal(fold_key, (C, C), jnp.float32), -4.0, 4.0) * scale_size
    queries = jnp.clip(jax.random.normal(fold_query, (C, C), jnp.float32), -4.0, 4.0) * scale_size
    return (queries, extra_noise)


def draw_w_query(key, part):
    return query_key_pair(key)[0].astype(jnp.bfloat16)


def draw_w_key(key, part):
    return query_key_pair(key)[1].astype(jnp.bfloat16)


def block_scale(rng, dims, cuts, least, top_value):
    loudness = 1.0
    for position, shards_of in cuts:
        heights = jax.random.uniform(jax.random.fold_in(jax.random.fold_in(rng, 6), position), (shards_of,), jnp.float32, least / len(cuts), top_value / len(cuts))
        loudness = loudness * jnp.repeat(jnp.exp(heights), dims[position] // shards_of).reshape((-1,) + (1,) * (len(dims) - 1 - position))
    return loudness


def gaussian(rng, dims, deviation, bound, shards=(), kind=jnp.bfloat16):
    result = deviation * jax.random.normal(rng, dims, jnp.float32)
    if shards:
        result = result * block_scale(rng, dims, shards, -0.22, 0.18)
    return jnp.clip(result, -bound, bound).astype(kind)


def setup_inputs(seed: int = 0, part: int = 0) -> dict:
    seeds = jax.random.split(jax.random.key(seed), 15)
    own_keys = jax.random.split(jax.random.fold_in(seeds[14], part), 15)
    latent = draw_latent(jax.random.fold_in(jax.random.fold_in(seeds[14], part), 71), part)
    norm1_gain = jnp.clip(1.0 + 0.1 * jax.random.normal(seeds[1], (C,), jnp.float32), 0.5, 1.5)
    norm1_bias = gaussian(seeds[2], (C,), 0.3, 1.2, ((0, 2),), jnp.float32)
    conv_weight = gaussian(seeds[3], (TAPS * C, C), (TAPS * C) ** -0.5, 0.0546875, ((0, 4), (1, 2)))
    conv_bias = gaussian(seeds[4], (C,), 0.3, 1.2, ((0, 2),), jnp.float32)
    norm2_gain = jnp.clip(1.0 + 0.1 * jax.random.normal(seeds[5], (C,), jnp.float32), 0.5, 1.5)
    norm2_bias = gaussian(seeds[6], (C,), 0.3, 1.2, ((0, 2),), jnp.float32)
    w_query = draw_w_query(jax.random.fold_in(seeds[14], 71), part)
    b_query = gaussian(seeds[8], (C,), 0.3, 1.2, (), jnp.float32)
    w_key = draw_w_key(jax.random.fold_in(seeds[14], 71), part)
    w_value = gaussian(seeds[10], (C, C), C ** -0.5, 0.25)
    b_value = gaussian(seeds[11], (C,), 0.3, 1.2, (), jnp.float32)
    w_out = gaussian(seeds[12], (C, C), C ** -0.5, 0.25)
    b_out = gaussian(seeds[13], (C,), 0.3, 1.2, (), jnp.float32)
    return {"latent": latent, "norm1_gain": norm1_gain, "norm1_bias": norm1_bias, "conv_weight": conv_weight, "conv_bias": conv_bias, "norm2_gain": norm2_gain, "norm2_bias": norm2_bias, "w_query": w_query, "b_query": b_query, "w_key": w_key, "w_value": w_value, "b_value": b_value, "w_out": w_out, "b_out": b_out}


EPSILON = 1e-06

def group_norm(values, gain, bias, axes):
    full_shape = values.shape
    grouped = values.astype(jnp.float32).reshape(full_shape[:-1] + (GROUPS, full_shape[-1] // GROUPS))
    group_mean = lax.optimization_barrier(jnp.mean(grouped, axis=axes, keepdims=True))
    centered = grouped - group_mean
    group_var = lax.optimization_barrier(jnp.mean(centered * centered, axis=axes, keepdims=True))
    return (centered * lax.rsqrt(group_var + EPSILON)).reshape(full_shape) * gain + bias

def causal_conv(activated, conv_weight, conv_bias):
    padded = jnp.pad(activated, ((2, 0), (1, 1), (1, 1), (0, 0)), mode='edge')
    accumulated = jnp.zeros((FRAMES * H * W, C), jnp.float32)
    tap_index = 0
    for frame_step in range(3):
        for row_step in range(3):
            for column_step in range(3):
                window = padded[frame_step:frame_step + FRAMES, row_step:row_step + H, column_step:column_step + W].reshape(FRAMES * H * W, C)
                accumulated = accumulated + jnp.dot(window, conv_weight[tap_index * C:(tap_index + 1) * C], preferred_element_type=jnp.float32)
                tap_index = tap_index + 1
    return (accumulated + conv_bias).reshape(FRAMES, H, W, C)

def frame_attention(single_frame, w_query, b_query, w_key, w_value, b_value, w_out, b_out):
    flattened = single_frame.reshape(H * W, C)
    queries = (jnp.dot(flattened, w_query, preferred_element_type=jnp.float32) + b_query).astype(jnp.bfloat16)
    keys = jnp.dot(flattened, w_key, preferred_element_type=jnp.float32).astype(jnp.bfloat16)
    values = (jnp.dot(flattened, w_value, preferred_element_type=jnp.float32) + b_value).astype(jnp.bfloat16)
    scores = jnp.dot(queries, keys.T, preferred_element_type=jnp.float32) * C ** (-0.5)
    row_peak = lax.optimization_barrier(jnp.max(scores, axis=1, keepdims=True))
    weights = jnp.exp(scores - row_peak)
    weight_sum = lax.optimization_barrier(jnp.sum(weights, axis=1, keepdims=True))
    attended = (jnp.dot(weights.astype(jnp.bfloat16), values, preferred_element_type=jnp.float32) / weight_sum).astype(jnp.bfloat16)
    branch = (jnp.dot(attended, w_out, preferred_element_type=jnp.float32) + b_out).astype(jnp.bfloat16)
    return branch.reshape(H, W, C)

def reference(latent, norm1_gain, norm1_bias, conv_weight, conv_bias, norm2_gain, norm2_bias, w_query, b_query, w_key, w_value, b_value, w_out, b_out):
    activated = jax.nn.silu(group_norm(latent, norm1_gain, norm1_bias, (0, 1, 2, 4))).astype(jnp.bfloat16)
    middle = (latent.astype(jnp.float32) + causal_conv(activated, conv_weight, conv_bias)).astype(jnp.bfloat16)
    normed = group_norm(middle, norm2_gain, norm2_bias, (1, 2, 4)).astype(jnp.bfloat16)
    branch = lax.map(lambda single_frame: frame_attention(single_frame, w_query, b_query, w_key, w_value, b_value, w_out, b_out), normed)
    return (middle.astype(jnp.float32) + branch.astype(jnp.float32)).astype(jnp.bfloat16)
```

```python
import jax
import jax.numpy as jnp
from jax import lax
from jax.sharding import PartitionSpec as P

C = 512
GROUPS = 32


EPSILON = 1e-06


def group_stats(values, group_size, axes):
    grouped = values.astype(jnp.float32).reshape(
        values.shape[:-1] + (values.shape[-1] // group_size, group_size)
    )
    group_mean = jnp.mean(grouped, axis=axes, keepdims=True)
    centered = grouped - group_mean
    group_var = jnp.mean(centered * centered, axis=axes, keepdims=True)
    return group_mean, group_var


def apply_norm(values, group_mean, group_var, group_size):
    grouped = values.astype(jnp.float32).reshape(
        values.shape[:-1] + (values.shape[-1] // group_size, group_size)
    )
    return ((grouped - group_mean) * lax.rsqrt(group_var + EPSILON)).reshape(values.shape)


def edge_pad(cells, dim, before, after):
    size = cells.shape[dim]
    parts = [lax.slice_in_dim(cells, 0, 1, axis=dim)] * before + [cells]
    parts += [lax.slice_in_dim(cells, size - 1, size, axis=dim)] * after
    return jnp.concatenate(parts, axis=dim)


def local(
    latent,
    norm1_gain,
    norm1_bias,
    conv_weight,
    conv_bias,
    norm2_gain,
    norm2_bias,
    w_query,
    b_query,
    w_key,
    w_value,
    b_value,
    w_out,
    b_out,
):
    frames, rows_here, columns, channels = latent.shape
    group_size = C // GROUPS
    time_count = lax.axis_size("tm")
    row_count = lax.axis_size("rows")
    chan_count = lax.axis_size("chan")
    time_place = lax.axis_index("tm")
    row_place = lax.axis_index("rows")
    chan_place = lax.axis_index("chan")
    all_rows = rows_here * row_count

    gathered = lax.all_gather(latent, ("tm", "rows", "chan"), axis=0, tiled=False)
    gathered = gathered.reshape(
        (time_count, row_count, chan_count, frames, rows_here, columns, channels)
    )
    clip = jnp.transpose(gathered, (0, 3, 1, 4, 5, 2, 6)).reshape(
        (time_count * frames, all_rows, columns, chan_count * channels)
    )

    mean1, var1 = group_stats(clip, group_size, (0, 1, 2, 4))
    frame_index = jnp.clip(
        time_place * frames - 2 + jnp.arange(frames + 2), 0, time_count * frames - 1
    )
    segment = jnp.take(clip, frame_index, axis=0)
    gain1 = lax.all_gather(norm1_gain, "chan", axis=0, tiled=True)
    bias1 = lax.all_gather(norm1_bias, "chan", axis=0, tiled=True)
    activated = jax.nn.silu(apply_norm(segment, mean1, var1, group_size) * gain1 + bias1).astype(
        jnp.bfloat16
    )
    padded = edge_pad(edge_pad(activated, 1, 1, 1), 2, 1, 1)

    block_rows = conv_weight.shape[0]
    start = row_place * block_rows
    first_tap = start // C
    offset = start % C
    span = max(
        (place * block_rows + block_rows - 1) // C - (place * block_rows) // C + 1
        for place in range(row_count)
    )
    out_channels = conv_weight.shape[1]
    placed = lax.dynamic_update_slice(
        jnp.zeros((span * C, out_channels), conv_weight.dtype), conv_weight, (offset, 0)
    )
    windows = []
    for step in range(span):
        tap = jnp.minimum(first_tap + step, (block_rows * row_count) // C - 1)
        windows.append(
            lax.dynamic_slice(
                padded,
                (tap // 9, (tap // 3) % 3, tap % 3, 0),
                (frames, all_rows, columns, C),
            ).reshape(-1, C)
        )
    patches = jnp.concatenate(windows, axis=1)
    partial = jnp.dot(patches, placed, preferred_element_type=jnp.float32)
    convolved = lax.psum(partial, "rows").reshape(frames, all_rows, columns, out_channels)

    own = lax.dynamic_slice(
        clip,
        (time_place * frames, 0, 0, chan_place * out_channels),
        (frames, all_rows, columns, out_channels),
    )
    middle = (own.astype(jnp.float32) + convolved + conv_bias).astype(jnp.bfloat16)

    mean2, var2 = group_stats(middle, group_size, (1, 2, 4))
    normed = (apply_norm(middle, mean2, var2, group_size) * norm2_gain + norm2_bias).astype(
        jnp.bfloat16
    )
    features = lax.all_gather(normed, "chan", axis=3, tiled=True)

    tokens = all_rows * columns
    local_tokens = rows_here * columns
    feature_rows = features.reshape(frames, tokens, C)
    own_rows = lax.dynamic_slice(
        features, (0, row_place * rows_here, 0, 0), (frames, rows_here, columns, C)
    ).reshape(-1, C)
    queries = (
        (jnp.dot(own_rows, w_query, preferred_element_type=jnp.float32) + b_query)
        .astype(jnp.bfloat16)
        .reshape(frames, local_tokens, C)
    )
    flat = feature_rows.reshape(-1, C)
    keys = (
        jnp.dot(flat, w_key, preferred_element_type=jnp.float32)
        .astype(jnp.bfloat16)
        .reshape(frames, tokens, C)
    )
    values = (
        (jnp.dot(flat, w_value, preferred_element_type=jnp.float32) + b_value)
        .astype(jnp.bfloat16)
        .reshape(frames, tokens, C)
    )
    scores = jnp.einsum("fqc,fkc->fqk", queries, keys, preferred_element_type=jnp.float32) * (
        C ** (-0.5)
    )
    row_peak = jnp.max(scores, axis=2, keepdims=True)
    weights = jnp.exp(scores - row_peak)
    weight_sum = jnp.sum(weights, axis=2, keepdims=True)
    attended = (
        jnp.einsum(
            "fqk,fkc->fqc",
            weights.astype(jnp.bfloat16),
            values,
            preferred_element_type=jnp.float32,
        )
        / weight_sum
    ).astype(jnp.bfloat16)
    out_block = lax.dynamic_slice(w_out, (0, chan_place * out_channels), (C, out_channels))
    out_bias = lax.dynamic_slice(b_out, (chan_place * out_channels,), (out_channels,))
    branch = (
        (jnp.dot(attended.reshape(-1, C), out_block, preferred_element_type=jnp.float32) + out_bias)
        .astype(jnp.bfloat16)
        .reshape(frames, rows_here, columns, out_channels)
    )
    own_middle = lax.dynamic_slice(
        middle, (0, row_place * rows_here, 0, 0), (frames, rows_here, columns, out_channels)
    )
    return (own_middle.astype(jnp.float32) + branch.astype(jnp.float32)).astype(jnp.bfloat16)


def solution(mesh):
    in_specs = (
        P(("clips", "tm"), "rows", None, "chan"),
        P("chan"),
        P("chan"),
        P("rows", "chan"),
        P("chan"),
        P("chan"),
        P("chan"),
        P(),
        P(),
        P(),
        P(),
        P(),
        P(),
        P(),
    )
    out_specs = P(("clips", "tm"), "rows", None, "chan")
    return jax.shard_map(local, mesh=mesh, in_specs=in_specs, out_specs=out_specs, check_vma=False)
```

```python
import jax
import jax.numpy as jnp
from jax import lax
from jax.sharding import PartitionSpec as P

C = 512
GROUPS = 32


EPSILON = 1e-06


def group_stats(values, group_size, axes):
    grouped = values.astype(jnp.float32).reshape(
        values.shape[:-1] + (values.shape[-1] // group_size, group_size)
    )
    group_mean = jnp.mean(grouped, axis=axes, keepdims=True)
    centered = grouped - group_mean
    group_var = jnp.mean(centered * centered, axis=axes, keepdims=True)
    return group_mean, group_var


def apply_norm(values, group_mean, group_var, group_size):
    grouped = values.astype(jnp.float32).reshape(
        values.shape[:-1] + (values.shape[-1] // group_size, group_size)
    )
    return ((grouped - group_mean) * lax.rsqrt(group_var + EPSILON)).reshape(values.shape)


def edge_pad(cells, dim, before, after):
    size = cells.shape[dim]
    parts = [lax.slice_in_dim(cells, 0, 1, axis=dim)] * before + [cells]
    parts += [lax.slice_in_dim(cells, size - 1, size, axis=dim)] * after
    return jnp.concatenate(parts, axis=dim)


def local(
    latent,
    norm1_gain,
    norm1_bias,
    conv_weight,
    conv_bias,
    norm2_gain,
    norm2_bias,
    w_query,
    b_query,
    w_key,
    w_value,
    b_value,
    w_out,
    b_out,
):
    frames, rows_here, columns, channels = latent.shape
    group_size = C // GROUPS
    time_count = lax.axis_size("tm")
    row_count = lax.axis_size("rows")
    chan_count = lax.axis_size("chan")
    time_place = lax.axis_index("tm")
    row_place = lax.axis_index("rows")
    chan_place = lax.axis_index("chan")
    all_rows = rows_here * row_count

    group = ("rows", "tm", "chan")
    copies = jnp.broadcast_to(latent[None], (row_count * time_count * chan_count,) + latent.shape)
    gathered = lax.all_to_all(copies, group, 0, 0, tiled=True).reshape(
        (row_count, time_count, chan_count, frames, rows_here, columns, channels)
    )
    clip = jnp.transpose(gathered, (1, 3, 0, 4, 5, 2, 6)).reshape(
        (time_count * frames, all_rows, columns, chan_count * channels)
    )

    mean1, var1 = group_stats(clip, group_size, (0, 1, 2, 4))
    frame_index = jnp.clip(
        time_place * frames - 2 + jnp.arange(frames + 2), 0, time_count * frames - 1
    )
    segment = jnp.take(clip, frame_index, axis=0)
    scales = lax.all_gather(
        jnp.stack([norm1_gain, norm1_bias, norm2_gain, norm2_bias]), "chan", axis=1, tiled=True
    )
    gain1, bias1, gain2, bias2 = scales[0], scales[1], scales[2], scales[3]
    activated = jax.nn.silu(apply_norm(segment, mean1, var1, group_size) * gain1 + bias1).astype(
        jnp.bfloat16
    )
    padded = edge_pad(edge_pad(activated, 1, 1, 1), 2, 1, 1)

    block_rows = conv_weight.shape[0]
    start = row_place * block_rows
    first_tap = start // C
    offset = start % C
    span = max(
        (place * block_rows + block_rows - 1) // C - (place * block_rows) // C + 1
        for place in range(row_count)
    )
    out_channels = conv_weight.shape[1]
    placed = lax.dynamic_update_slice(
        jnp.zeros((span * C, out_channels), conv_weight.dtype), conv_weight, (offset, 0)
    )
    windows = []
    for step in range(span):
        tap = jnp.minimum(first_tap + step, (block_rows * row_count) // C - 1)
        windows.append(
            lax.dynamic_slice(
                padded,
                (tap // 9, (tap // 3) % 3, tap % 3, 0),
                (frames, all_rows, columns, C),
            ).reshape(-1, C)
        )
    patches = jnp.concatenate(windows, axis=1)
    partial = jnp.dot(patches, placed, preferred_element_type=jnp.float32)
    pieces = partial.reshape(frames, row_count, rows_here, columns, out_channels)
    convolved = jnp.sum(lax.all_to_all(pieces, "rows", 1, 1, tiled=True), axis=1)
    own_middle = (latent.astype(jnp.float32) + convolved + conv_bias).astype(jnp.bfloat16)

    spread = jnp.broadcast_to(own_middle[None], (row_count * chan_count,) + own_middle.shape)
    middle = lax.all_to_all(spread, ("rows", "chan"), 0, 0, tiled=True).reshape(
        (row_count, chan_count, frames, rows_here, columns, out_channels)
    )
    middle = jnp.transpose(middle, (2, 0, 3, 4, 1, 5)).reshape(frames, all_rows, columns, C)
    mean2, var2 = group_stats(middle, group_size, (1, 2, 4))
    features = (apply_norm(middle, mean2, var2, group_size) * gain2 + bias2).astype(jnp.bfloat16)

    tokens = all_rows * columns
    local_tokens = rows_here * columns
    feature_rows = features.reshape(frames, tokens, C)
    own_rows = lax.dynamic_slice(
        features, (0, row_place * rows_here, 0, 0), (frames, rows_here, columns, C)
    ).reshape(-1, C)
    queries = (
        (jnp.dot(own_rows, w_query, preferred_element_type=jnp.float32) + b_query)
        .astype(jnp.bfloat16)
        .reshape(frames, local_tokens, C)
    )
    flat = feature_rows.reshape(-1, C)
    keys = (
        jnp.dot(flat, w_key, preferred_element_type=jnp.float32)
        .astype(jnp.bfloat16)
        .reshape(frames, tokens, C)
    )
    values = (
        (jnp.dot(flat, w_value, preferred_element_type=jnp.float32) + b_value)
        .astype(jnp.bfloat16)
        .reshape(frames, tokens, C)
    )
    scores = jnp.einsum("fqc,fkc->fqk", queries, keys, preferred_element_type=jnp.float32) * (
        C ** (-0.5)
    )
    row_peak = jnp.max(scores, axis=2, keepdims=True)
    weights = jnp.exp(scores - row_peak)
    weight_sum = jnp.sum(weights, axis=2, keepdims=True)
    attended = (
        jnp.einsum(
            "fqk,fkc->fqc",
            weights.astype(jnp.bfloat16),
            values,
            preferred_element_type=jnp.float32,
        )
        / weight_sum
    ).astype(jnp.bfloat16)
    out_block = lax.dynamic_slice(w_out, (0, chan_place * out_channels), (C, out_channels))
    out_bias = lax.dynamic_slice(b_out, (chan_place * out_channels,), (out_channels,))
    branch = (
        (jnp.dot(attended.reshape(-1, C), out_block, preferred_element_type=jnp.float32) + out_bias)
        .astype(jnp.bfloat16)
        .reshape(frames, rows_here, columns, out_channels)
    )
    return (own_middle.astype(jnp.float32) + branch.astype(jnp.float32)).astype(jnp.bfloat16)


def solution(mesh):
    in_specs = (
        P(("clips", "tm"), "rows", None, "chan"),
        P("chan"),
        P("chan"),
        P("rows", "chan"),
        P("chan"),
        P("chan"),
        P("chan"),
        P(),
        P(),
        P(),
        P(),
        P(),
        P(),
        P(),
    )
    out_specs = P(("clips", "tm"), "rows", None, "chan")
    return jax.shard_map(local, mesh=mesh, in_specs=in_specs, out_specs=out_specs, check_vma=False)
```

```python
import jax
import jax.numpy as jnp
from jax import lax
from jax.sharding import PartitionSpec as P

C = 512
GROUPS = 32


EPSILON = 1e-06


def group_stats(values, group_size, axes):
    grouped = values.astype(jnp.float32).reshape(
        values.shape[:-1] + (values.shape[-1] // group_size, group_size)
    )
    group_mean = jnp.mean(grouped, axis=axes, keepdims=True)
    centered = grouped - group_mean
    group_var = jnp.mean(centered * centered, axis=axes, keepdims=True)
    return group_mean, group_var


def apply_norm(values, group_mean, group_var, group_size):
    grouped = values.astype(jnp.float32).reshape(
        values.shape[:-1] + (values.shape[-1] // group_size, group_size)
    )
    return ((grouped - group_mean) * lax.rsqrt(group_var + EPSILON)).reshape(values.shape)


def edge_pad(cells, dim, before, after):
    size = cells.shape[dim]
    parts = [lax.slice_in_dim(cells, 0, 1, axis=dim)] * before + [cells]
    parts += [lax.slice_in_dim(cells, size - 1, size, axis=dim)] * after
    return jnp.concatenate(parts, axis=dim)


def local(
    latent,
    norm1_gain,
    norm1_bias,
    conv_weight,
    conv_bias,
    norm2_gain,
    norm2_bias,
    w_query,
    b_query,
    w_key,
    w_value,
    b_value,
    w_out,
    b_out,
):
    frames, rows_here, columns, channels = latent.shape
    group_size = C // GROUPS
    time_count = lax.axis_size("tm")
    row_count = lax.axis_size("rows")
    chan_count = lax.axis_size("chan")
    time_place = lax.axis_index("tm")
    row_place = lax.axis_index("rows")
    chan_place = lax.axis_index("chan")
    all_rows = rows_here * row_count

    group = ("rows", "tm")
    copies = jnp.broadcast_to(latent[None], (row_count * time_count,) + latent.shape)
    gathered = lax.all_to_all(copies, group, 0, 0, tiled=True)
    gathered = lax.all_gather(gathered, "chan", axis=4, tiled=True).reshape(
        (row_count, time_count, frames, rows_here, columns, chan_count * channels)
    )
    clip = jnp.transpose(gathered, (1, 2, 0, 3, 4, 5)).reshape(
        (time_count * frames, all_rows, columns, chan_count * channels)
    )

    mean1, var1 = group_stats(clip, group_size, (0, 1, 2, 4))
    frame_index = jnp.clip(
        time_place * frames - 2 + jnp.arange(frames + 2), 0, time_count * frames - 1
    )
    segment = jnp.take(clip, frame_index, axis=0)
    scales = lax.all_gather(
        jnp.stack([norm1_gain, norm1_bias, norm2_gain, norm2_bias]), "chan", axis=1, tiled=True
    )
    gain1, bias1, gain2, bias2 = scales[0], scales[1], scales[2], scales[3]
    activated = jax.nn.silu(apply_norm(segment, mean1, var1, group_size) * gain1 + bias1).astype(
        jnp.bfloat16
    )
    padded = edge_pad(edge_pad(activated, 1, 1, 1), 2, 1, 1)

    block_rows = conv_weight.shape[0]
    start = row_place * block_rows
    first_tap = start // C
    offset = start % C
    span = max(
        (place * block_rows + block_rows - 1) // C - (place * block_rows) // C + 1
        for place in range(row_count)
    )
    out_channels = conv_weight.shape[1]
    placed = lax.dynamic_update_slice(
        jnp.zeros((span * C, out_channels), conv_weight.dtype), conv_weight, (offset, 0)
    )
    windows = []
    for step in range(span):
        tap = jnp.minimum(first_tap + step, (block_rows * row_count) // C - 1)
        windows.append(
            lax.dynamic_slice(
                padded,
                (tap // 9, (tap // 3) % 3, tap % 3, 0),
                (frames, all_rows, columns, C),
            ).reshape(-1, C)
        )
    patches = jnp.concatenate(windows, axis=1)
    partial = jnp.dot(patches, placed, preferred_element_type=jnp.float32)
    pieces = partial.reshape(frames, row_count, rows_here, columns, out_channels)
    convolved = jnp.sum(lax.all_to_all(pieces, "rows", 1, 1, tiled=True), axis=1)
    own_middle = (latent.astype(jnp.float32) + convolved + conv_bias).astype(jnp.bfloat16)

    spread = jnp.tile(own_middle, (1, row_count, 1, 1))
    middle = lax.all_to_all(spread, "rows", 1, 1, tiled=True)
    middle = lax.all_gather(middle, "chan", axis=3, tiled=True)
    mean2, var2 = group_stats(middle, group_size, (1, 2, 4))
    features = (apply_norm(middle, mean2, var2, group_size) * gain2 + bias2).astype(jnp.bfloat16)

    tokens = all_rows * columns
    local_tokens = rows_here * columns
    feature_rows = features.reshape(frames, tokens, C)
    own_rows = lax.dynamic_slice(
        features, (0, row_place * rows_here, 0, 0), (frames, rows_here, columns, C)
    ).reshape(-1, C)
    queries = (
        (jnp.dot(own_rows, w_query, preferred_element_type=jnp.float32) + b_query)
        .astype(jnp.bfloat16)
        .reshape(frames, local_tokens, C)
    )
    flat = feature_rows.reshape(-1, C)
    keys = (
        jnp.dot(flat, w_key, preferred_element_type=jnp.float32)
        .astype(jnp.bfloat16)
        .reshape(frames, tokens, C)
    )
    values = (
        (jnp.dot(flat, w_value, preferred_element_type=jnp.float32) + b_value)
        .astype(jnp.bfloat16)
        .reshape(frames, tokens, C)
    )
    scores = jnp.einsum("fqc,fkc->fqk", queries, keys, preferred_element_type=jnp.float32) * (
        C ** (-0.5)
    )
    row_peak = jnp.max(scores, axis=2, keepdims=True)
    weights = jnp.exp(scores - row_peak)
    weight_sum = jnp.sum(weights, axis=2, keepdims=True)
    attended = (
        jnp.einsum(
            "fqk,fkc->fqc",
            weights.astype(jnp.bfloat16),
            values,
            preferred_element_type=jnp.float32,
        )
        / weight_sum
    ).astype(jnp.bfloat16)
    out_block = lax.dynamic_slice(w_out, (0, chan_place * out_channels), (C, out_channels))
    out_bias = lax.dynamic_slice(b_out, (chan_place * out_channels,), (out_channels,))
    branch = (
        (jnp.dot(attended.reshape(-1, C), out_block, preferred_element_type=jnp.float32) + out_bias)
        .astype(jnp.bfloat16)
        .reshape(frames, rows_here, columns, out_channels)
    )
    return (own_middle.astype(jnp.float32) + branch.astype(jnp.float32)).astype(jnp.bfloat16)


def solution(mesh):
    in_specs = (
        P(("clips", "tm"), "rows", None, "chan"),
        P("chan"),
        P("chan"),
        P("rows", "chan"),
        P("chan"),
        P("chan"),
        P("chan"),
        P(),
        P(),
        P(),
        P(),
        P(),
        P(),
        P(),
    )
    out_specs = P(("clips", "tm"), "rows", None, "chan")
    return jax.shard_map(local, mesh=mesh, in_specs=in_specs, out_specs=out_specs, check_vma=False)
```

```python
import jax
import jax.numpy as jnp
from jax import lax
from jax.sharding import PartitionSpec as P

C = 512
GROUPS = 32


EPSILON = 1e-06


def group_stats(values, group_size, axes):
    grouped = values.astype(jnp.float32).reshape(
        values.shape[:-1] + (values.shape[-1] // group_size, group_size)
    )
    group_mean = jnp.mean(grouped, axis=axes, keepdims=True)
    centered = grouped - group_mean
    group_var = jnp.mean(centered * centered, axis=axes, keepdims=True)
    return group_mean, group_var


def apply_norm(values, group_mean, group_var, group_size):
    grouped = values.astype(jnp.float32).reshape(
        values.shape[:-1] + (values.shape[-1] // group_size, group_size)
    )
    return ((grouped - group_mean) * lax.rsqrt(group_var + EPSILON)).reshape(values.shape)


def edge_pad(cells, dim, before, after):
    size = cells.shape[dim]
    parts = [lax.slice_in_dim(cells, 0, 1, axis=dim)] * before + [cells]
    parts += [lax.slice_in_dim(cells, size - 1, size, axis=dim)] * after
    return jnp.concatenate(parts, axis=dim)


def chan_gather(cells, axis):
    count = lax.axis_size("chan")
    place = lax.axis_index("chan")
    received = [cells] + [
        lax.ppermute(cells, "chan", [(i, (i + shift) % count) for i in range(count)])
        for shift in range(1, count)
    ]
    blocks = []
    for position in range(count):
        chosen = received[0]
        for shift in range(1, count):
            chosen = jnp.where((place - position) % count == shift, received[shift], chosen)
        blocks.append(chosen)
    return jnp.concatenate(blocks, axis=axis)


def local(
    latent,
    norm1_gain,
    norm1_bias,
    conv_weight,
    conv_bias,
    norm2_gain,
    norm2_bias,
    w_query,
    b_query,
    w_key,
    w_value,
    b_value,
    w_out,
    b_out,
):
    frames, rows_here, columns, channels = latent.shape
    group_size = C // GROUPS
    time_count = lax.axis_size("tm")
    row_count = lax.axis_size("rows")
    chan_count = lax.axis_size("chan")
    time_place = lax.axis_index("tm")
    row_place = lax.axis_index("rows")
    chan_place = lax.axis_index("chan")
    all_rows = rows_here * row_count

    group = ("rows", "tm")
    copies = jnp.broadcast_to(latent[None], (row_count * time_count,) + latent.shape)
    gathered = lax.all_to_all(copies, group, 0, 0, tiled=True)
    gathered = chan_gather(gathered, 4).reshape(
        (row_count, time_count, frames, rows_here, columns, chan_count * channels)
    )
    clip = jnp.transpose(gathered, (1, 2, 0, 3, 4, 5)).reshape(
        (time_count * frames, all_rows, columns, chan_count * channels)
    )

    mean1, var1 = group_stats(clip, group_size, (0, 1, 2, 4))
    frame_index = jnp.clip(
        time_place * frames - 2 + jnp.arange(frames + 2), 0, time_count * frames - 1
    )
    segment = jnp.take(clip, frame_index, axis=0)
    scales = chan_gather(jnp.stack([norm1_gain, norm1_bias, norm2_gain, norm2_bias]), 1)
    gain1, bias1, gain2, bias2 = scales[0], scales[1], scales[2], scales[3]
    activated = jax.nn.silu(apply_norm(segment, mean1, var1, group_size) * gain1 + bias1).astype(
        jnp.bfloat16
    )
    padded = edge_pad(edge_pad(activated, 1, 1, 1), 2, 1, 1)

    block_rows = conv_weight.shape[0]
    start = row_place * block_rows
    first_tap = start // C
    offset = start % C
    span = max(
        (place * block_rows + block_rows - 1) // C - (place * block_rows) // C + 1
        for place in range(row_count)
    )
    out_channels = conv_weight.shape[1]
    placed = lax.dynamic_update_slice(
        jnp.zeros((span * C, out_channels), conv_weight.dtype), conv_weight, (offset, 0)
    )
    windows = []
    for step in range(span):
        tap = jnp.minimum(first_tap + step, (block_rows * row_count) // C - 1)
        windows.append(
            lax.dynamic_slice(
                padded,
                (tap // 9, (tap // 3) % 3, tap % 3, 0),
                (frames, all_rows, columns, C),
            ).reshape(-1, C)
        )
    patches = jnp.concatenate(windows, axis=1)
    partial = jnp.dot(patches, placed, preferred_element_type=jnp.float32)
    pieces = partial.reshape(frames, row_count, rows_here, columns, out_channels)
    convolved = jnp.sum(lax.all_to_all(pieces, "rows", 1, 1, tiled=True), axis=1)
    own_middle = (latent.astype(jnp.float32) + convolved + conv_bias).astype(jnp.bfloat16)

    spread = jnp.tile(own_middle, (1, row_count, 1, 1))
    middle = lax.all_to_all(spread, "rows", 1, 1, tiled=True)
    middle = chan_gather(middle, 3)
    mean2, var2 = group_stats(middle, group_size, (1, 2, 4))
    features = (apply_norm(middle, mean2, var2, group_size) * gain2 + bias2).astype(jnp.bfloat16)

    tokens = all_rows * columns
    local_tokens = rows_here * columns
    feature_rows = features.reshape(frames, tokens, C)
    own_rows = lax.dynamic_slice(
        features, (0, row_place * rows_here, 0, 0), (frames, rows_here, columns, C)
    ).reshape(-1, C)
    queries = (
        (jnp.dot(own_rows, w_query, preferred_element_type=jnp.float32) + b_query)
        .astype(jnp.bfloat16)
        .reshape(frames, local_tokens, C)
    )
    flat = feature_rows.reshape(-1, C)
    keys = (
        jnp.dot(flat, w_key, preferred_element_type=jnp.float32)
        .astype(jnp.bfloat16)
        .reshape(frames, tokens, C)
    )
    values = (
        (jnp.dot(flat, w_value, preferred_element_type=jnp.float32) + b_value)
        .astype(jnp.bfloat16)
        .reshape(frames, tokens, C)
    )
    scores = jnp.einsum("fqc,fkc->fqk", queries, keys, preferred_element_type=jnp.float32) * (
        C ** (-0.5)
    )
    row_peak = jnp.max(scores, axis=2, keepdims=True)
    weights = jnp.exp(scores - row_peak)
    weight_sum = jnp.sum(weights, axis=2, keepdims=True)
    attended = (
        jnp.einsum(
            "fqk,fkc->fqc",
            weights.astype(jnp.bfloat16),
            values,
            preferred_element_type=jnp.float32,
        )
        / weight_sum
    ).astype(jnp.bfloat16)
    out_block = lax.dynamic_slice(w_out, (0, chan_place * out_channels), (C, out_channels))
    out_bias = lax.dynamic_slice(b_out, (chan_place * out_channels,), (out_channels,))
    branch = (
        (jnp.dot(attended.reshape(-1, C), out_block, preferred_element_type=jnp.float32) + out_bias)
        .astype(jnp.bfloat16)
        .reshape(frames, rows_here, columns, out_channels)
    )
    return (own_middle.astype(jnp.float32) + branch.astype(jnp.float32)).astype(jnp.bfloat16)


def solution(mesh):
    in_specs = (
        P(("clips", "tm"), "rows", None, "chan"),
        P("chan"),
        P("chan"),
        P("rows", "chan"),
        P("chan"),
        P("chan"),
        P("chan"),
        P(),
        P(),
        P(),
        P(),
        P(),
        P(),
        P(),
    )
    out_specs = P(("clips", "tm"), "rows", None, "chan")
    return jax.shard_map(local, mesh=mesh, in_specs=in_specs, out_specs=out_specs, check_vma=False)
```

```python
import jax
import jax.numpy as jnp
from jax import lax
from jax.sharding import PartitionSpec as P

C = 512
GROUPS = 32


EPSILON = 1e-06


def group_stats(values, group_size, axes):
    grouped = values.astype(jnp.float32).reshape(
        values.shape[:-1] + (values.shape[-1] // group_size, group_size)
    )
    group_mean = jnp.mean(grouped, axis=axes, keepdims=True)
    centered = grouped - group_mean
    group_var = jnp.mean(centered * centered, axis=axes, keepdims=True)
    return group_mean, group_var


def apply_norm(values, group_mean, group_var, group_size):
    grouped = values.astype(jnp.float32).reshape(
        values.shape[:-1] + (values.shape[-1] // group_size, group_size)
    )
    return ((grouped - group_mean) * lax.rsqrt(group_var + EPSILON)).reshape(values.shape)


def edge_pad(cells, dim, before, after):
    size = cells.shape[dim]
    parts = [lax.slice_in_dim(cells, 0, 1, axis=dim)] * before + [cells]
    parts += [lax.slice_in_dim(cells, size - 1, size, axis=dim)] * after
    return jnp.concatenate(parts, axis=dim)


def chan_halves(cells):
    count = lax.axis_size("chan")
    return [cells] + [
        lax.ppermute(cells, "chan", [(i, (i + shift) % count) for i in range(count)])
        for shift in range(1, count)
    ]


def half_rows(weight, shift, width):
    count = lax.axis_size("chan")
    source = (lax.axis_index("chan") - shift) % count
    return lax.dynamic_slice_in_dim(weight, source * width, width, axis=0)


def split_dot(halves, weight, width):
    total = None
    for shift, half in enumerate(halves):
        term = jnp.dot(half, half_rows(weight, shift, width), preferred_element_type=jnp.float32)
        total = term if total is None else total + term
    return total


def local(
    latent,
    norm1_gain,
    norm1_bias,
    conv_weight,
    conv_bias,
    norm2_gain,
    norm2_bias,
    w_query,
    b_query,
    w_key,
    w_value,
    b_value,
    w_out,
    b_out,
):
    frames, rows_here, columns, channels = latent.shape
    group_size = C // GROUPS
    time_count = lax.axis_size("tm")
    row_count = lax.axis_size("rows")
    chan_count = lax.axis_size("chan")
    time_place = lax.axis_index("tm")
    row_place = lax.axis_index("rows")
    chan_place = lax.axis_index("chan")
    all_rows = rows_here * row_count

    copies = jnp.broadcast_to(latent[None], (row_count * time_count,) + latent.shape)
    gathered = lax.all_to_all(copies, ("rows", "tm"), 0, 0, tiled=True).reshape(
        (row_count, time_count, frames, rows_here, columns, channels)
    )
    clip = jnp.transpose(gathered, (1, 2, 0, 3, 4, 5)).reshape(
        (time_count * frames, all_rows, columns, channels)
    )

    mean1, var1 = group_stats(clip, group_size, (0, 1, 2, 4))
    frame_index = jnp.clip(
        time_place * frames - 2 + jnp.arange(frames + 2), 0, time_count * frames - 1
    )
    segment = jnp.take(clip, frame_index, axis=0)
    activated = jax.nn.silu(
        apply_norm(segment, mean1, var1, group_size) * norm1_gain + norm1_bias
    ).astype(jnp.bfloat16)
    padded = edge_pad(edge_pad(activated, 1, 1, 1), 2, 1, 1)
    padded_halves = chan_halves(padded)

    block_rows = conv_weight.shape[0]
    start = row_place * block_rows
    first_tap = start // C
    offset = start % C
    span = max(
        (place * block_rows + block_rows - 1) // C - (place * block_rows) // C + 1
        for place in range(row_count)
    )
    out_channels = conv_weight.shape[1]
    placed = lax.dynamic_update_slice(
        jnp.zeros((span * C, out_channels), conv_weight.dtype), conv_weight, (offset, 0)
    ).reshape(span, chan_count, channels, out_channels)
    taps = (block_rows * row_count) // C
    partial = None
    for shift, half in enumerate(padded_halves):
        source = (chan_place - shift) % chan_count
        windows = []
        for step in range(span):
            tap = jnp.minimum(first_tap + step, taps - 1)
            windows.append(
                lax.dynamic_slice(
                    half,
                    (tap // 9, (tap // 3) % 3, tap % 3, 0),
                    (frames, all_rows, columns, channels),
                ).reshape(-1, channels)
            )
        patches = jnp.concatenate(windows, axis=1)
        block = lax.dynamic_index_in_dim(placed, source, axis=1, keepdims=False).reshape(
            span * channels, out_channels
        )
        term = jnp.dot(patches, block, preferred_element_type=jnp.float32)
        partial = term if partial is None else partial + term

    pieces = partial.reshape(frames, row_count, rows_here, columns, out_channels)
    convolved = jnp.sum(lax.all_to_all(pieces, "rows", 1, 1, tiled=True), axis=1)
    own_middle = (latent.astype(jnp.float32) + convolved + conv_bias).astype(jnp.bfloat16)

    middle = lax.all_to_all(jnp.tile(own_middle, (1, row_count, 1, 1)), "rows", 1, 1, tiled=True)
    mean2, var2 = group_stats(middle, group_size, (1, 2, 4))
    normed = (apply_norm(middle, mean2, var2, group_size) * norm2_gain + norm2_bias).astype(
        jnp.bfloat16
    )
    normed_halves = chan_halves(normed)

    tokens = all_rows * columns
    local_tokens = rows_here * columns
    own_rows = [
        lax.dynamic_slice_in_dim(half, row_place * rows_here, rows_here, axis=1).reshape(
            -1, channels
        )
        for half in normed_halves
    ]
    flat = [half.reshape(-1, channels) for half in normed_halves]
    queries = (
        (split_dot(own_rows, w_query, channels) + b_query)
        .astype(jnp.bfloat16)
        .reshape(frames, local_tokens, C)
    )
    keys = split_dot(flat, w_key, channels).astype(jnp.bfloat16).reshape(frames, tokens, C)
    values = (
        (split_dot(flat, w_value, channels) + b_value)
        .astype(jnp.bfloat16)
        .reshape(frames, tokens, C)
    )
    scores = jnp.einsum("fqc,fkc->fqk", queries, keys, preferred_element_type=jnp.float32) * (
        C ** (-0.5)
    )
    row_peak = jnp.max(scores, axis=2, keepdims=True)
    weights = jnp.exp(scores - row_peak)
    weight_sum = jnp.sum(weights, axis=2, keepdims=True)
    attended = (
        jnp.einsum(
            "fqk,fkc->fqc",
            weights.astype(jnp.bfloat16),
            values,
            preferred_element_type=jnp.float32,
        )
        / weight_sum
    ).astype(jnp.bfloat16)
    out_block = lax.dynamic_slice(w_out, (0, chan_place * out_channels), (C, out_channels))
    out_bias = lax.dynamic_slice(b_out, (chan_place * out_channels,), (out_channels,))
    branch = (
        (jnp.dot(attended.reshape(-1, C), out_block, preferred_element_type=jnp.float32) + out_bias)
        .astype(jnp.bfloat16)
        .reshape(frames, rows_here, columns, out_channels)
    )
    return (own_middle.astype(jnp.float32) + branch.astype(jnp.float32)).astype(jnp.bfloat16)


def solution(mesh):
    in_specs = (
        P(("clips", "tm"), "rows", None, "chan"),
        P("chan"),
        P("chan"),
        P("rows", "chan"),
        P("chan"),
        P("chan"),
        P("chan"),
        P(),
        P(),
        P(),
        P(),
        P(),
        P(),
        P(),
    )
    out_specs = P(("clips", "tm"), "rows", None, "chan")
    return jax.shard_map(local, mesh=mesh, in_specs=in_specs, out_specs=out_specs, check_vma=False)
```

```python
import jax
import jax.numpy as jnp
from jax import lax
from jax.sharding import PartitionSpec as P

C = 512
GROUPS = 32


EPSILON = 1e-06


def group_stats(values, group_size, axes):
    grouped = values.astype(jnp.float32).reshape(
        values.shape[:-1] + (values.shape[-1] // group_size, group_size)
    )
    group_mean = jnp.mean(grouped, axis=axes, keepdims=True)
    centered = grouped - group_mean
    group_var = jnp.mean(centered * centered, axis=axes, keepdims=True)
    return group_mean, group_var


def apply_norm(values, group_mean, group_var, group_size):
    grouped = values.astype(jnp.float32).reshape(
        values.shape[:-1] + (values.shape[-1] // group_size, group_size)
    )
    return ((grouped - group_mean) * lax.rsqrt(group_var + EPSILON)).reshape(values.shape)


def edge_pad(cells, dim, before, after):
    size = cells.shape[dim]
    parts = [lax.slice_in_dim(cells, 0, 1, axis=dim)] * before + [cells]
    parts += [lax.slice_in_dim(cells, size - 1, size, axis=dim)] * after
    return jnp.concatenate(parts, axis=dim)


def chan_halves(cells):
    count = lax.axis_size("chan")
    return [cells] + [
        lax.ppermute(cells, "chan", [(i, (i + shift) % count) for i in range(count)])
        for shift in range(1, count)
    ]


def half_rows(weight, shift, width):
    count = lax.axis_size("chan")
    source = (lax.axis_index("chan") - shift) % count
    return lax.dynamic_slice_in_dim(weight, source * width, width, axis=0)


def split_dot(halves, weight, width):
    total = None
    for shift, half in enumerate(halves):
        term = jnp.dot(half, half_rows(weight, shift, width), preferred_element_type=jnp.float32)
        total = term if total is None else total + term
    return total


def local(
    latent,
    norm1_gain,
    norm1_bias,
    conv_weight,
    conv_bias,
    norm2_gain,
    norm2_bias,
    w_query,
    b_query,
    w_key,
    w_value,
    b_value,
    w_out,
    b_out,
):
    frames, rows_here, columns, channels = latent.shape
    group_size = C // GROUPS
    time_count = lax.axis_size("tm")
    row_count = lax.axis_size("rows")
    chan_count = lax.axis_size("chan")
    time_place = lax.axis_index("tm")
    row_place = lax.axis_index("rows")
    chan_place = lax.axis_index("chan")
    all_rows = rows_here * row_count

    copies = jnp.broadcast_to(latent[None], (row_count * time_count,) + latent.shape)
    gathered = lax.all_to_all(copies, ("rows", "tm"), 0, 0, tiled=True).reshape(
        (row_count, time_count, frames, rows_here, columns, channels)
    )
    clip = jnp.transpose(gathered, (1, 2, 0, 3, 4, 5)).reshape(
        (time_count * frames, all_rows, columns, channels)
    )

    mean1, var1 = group_stats(clip, group_size, (0, 1, 2, 4))
    frame_index = jnp.clip(
        time_place * frames - 2 + jnp.arange(frames + 2), 0, time_count * frames - 1
    )
    segment = jnp.take(clip, frame_index, axis=0)
    activated = jax.nn.silu(
        apply_norm(segment, mean1, var1, group_size) * norm1_gain + norm1_bias
    ).astype(jnp.bfloat16)
    padded = edge_pad(edge_pad(activated, 1, 1, 1), 2, 1, 1)
    padded_halves = chan_halves(padded)

    block_rows = conv_weight.shape[0]
    start = row_place * block_rows
    first_tap = start // C
    offset = start % C
    span = max(
        (place * block_rows + block_rows - 1) // C - (place * block_rows) // C + 1
        for place in range(row_count)
    )
    out_channels = conv_weight.shape[1]
    placed = lax.dynamic_update_slice(
        jnp.zeros((span * C, out_channels), conv_weight.dtype), conv_weight, (offset, 0)
    ).reshape(span, chan_count, channels, out_channels)
    taps = (block_rows * row_count) // C
    partial = None
    for shift, half in enumerate(padded_halves):
        source = (chan_place - shift) % chan_count
        block = lax.dynamic_index_in_dim(placed, source, axis=1, keepdims=False)
        for step in range(span):
            tap = jnp.minimum(first_tap + step, taps - 1)
            window = lax.dynamic_slice(
                half,
                (tap // 9, (tap // 3) % 3, tap % 3, 0),
                (frames, all_rows, columns, channels),
            ).reshape(-1, channels)
            term = jnp.dot(window, block[step], preferred_element_type=jnp.float32)
            partial = term if partial is None else partial + term

    pieces = partial.reshape(frames, row_count, rows_here, columns, out_channels)
    convolved = jnp.sum(lax.all_to_all(pieces, "rows", 1, 1, tiled=True), axis=1)
    own_middle = (latent.astype(jnp.float32) + convolved + conv_bias).astype(jnp.bfloat16)

    middle = lax.all_to_all(jnp.tile(own_middle, (1, row_count, 1, 1)), "rows", 1, 1, tiled=True)
    mean2, var2 = group_stats(middle, group_size, (1, 2, 4))
    normed = (apply_norm(middle, mean2, var2, group_size) * norm2_gain + norm2_bias).astype(
        jnp.bfloat16
    )
    normed_halves = chan_halves(normed)

    tokens = all_rows * columns
    local_tokens = rows_here * columns
    own_rows = [
        lax.dynamic_slice_in_dim(half, row_place * rows_here, rows_here, axis=1).reshape(
            -1, channels
        )
        for half in normed_halves
    ]
    flat = [half.reshape(-1, channels) for half in normed_halves]
    queries = (
        (split_dot(own_rows, w_query, channels) + b_query)
        .astype(jnp.bfloat16)
        .reshape(frames, local_tokens, C)
    )
    keys = split_dot(flat, w_key, channels).astype(jnp.bfloat16).reshape(frames, tokens, C)
    values = (
        (split_dot(flat, w_value, channels) + b_value)
        .astype(jnp.bfloat16)
        .reshape(frames, tokens, C)
    )
    scores = jnp.einsum("fqc,fkc->fqk", queries, keys, preferred_element_type=jnp.float32) * (
        C ** (-0.5)
    )
    row_peak = jnp.max(scores, axis=2, keepdims=True)
    weights = jnp.exp(scores - row_peak)
    weight_sum = jnp.sum(weights, axis=2, keepdims=True)
    attended = (
        jnp.einsum(
            "fqk,fkc->fqc",
            weights.astype(jnp.bfloat16),
            values,
            preferred_element_type=jnp.float32,
        )
        / weight_sum
    ).astype(jnp.bfloat16)
    out_block = lax.dynamic_slice(w_out, (0, chan_place * out_channels), (C, out_channels))
    out_bias = lax.dynamic_slice(b_out, (chan_place * out_channels,), (out_channels,))
    branch = (
        (jnp.dot(attended.reshape(-1, C), out_block, preferred_element_type=jnp.float32) + out_bias)
        .astype(jnp.bfloat16)
        .reshape(frames, rows_here, columns, out_channels)
    )
    return (own_middle.astype(jnp.float32) + branch.astype(jnp.float32)).astype(jnp.bfloat16)


def solution(mesh):
    in_specs = (
        P(("clips", "tm"), "rows", None, "chan"),
        P("chan"),
        P("chan"),
        P("rows", "chan"),
        P("chan"),
        P("chan"),
        P("chan"),
        P(),
        P(),
        P(),
        P(),
        P(),
        P(),
        P(),
    )
    out_specs = P(("clips", "tm"), "rows", None, "chan")
    return jax.shard_map(local, mesh=mesh, in_specs=in_specs, out_specs=out_specs, check_vma=False)
```

```python
import jax
import jax.numpy as jnp
from jax import lax
from jax.sharding import PartitionSpec as P

C = 512
GROUPS = 32


EPSILON = 1e-06


def group_stats(values, group_size, axes):
    grouped = values.astype(jnp.float32).reshape(
        values.shape[:-1] + (values.shape[-1] // group_size, group_size)
    )
    group_mean = jnp.mean(grouped, axis=axes, keepdims=True)
    centered = grouped - group_mean
    group_var = jnp.mean(centered * centered, axis=axes, keepdims=True)
    return group_mean, group_var


def apply_norm(values, group_mean, group_var, group_size):
    grouped = values.astype(jnp.float32).reshape(
        values.shape[:-1] + (values.shape[-1] // group_size, group_size)
    )
    return ((grouped - group_mean) * lax.rsqrt(group_var + EPSILON)).reshape(values.shape)


def edge_pad(cells, dim, before, after):
    size = cells.shape[dim]
    parts = [lax.slice_in_dim(cells, 0, 1, axis=dim)] * before + [cells]
    parts += [lax.slice_in_dim(cells, size - 1, size, axis=dim)] * after
    return jnp.concatenate(parts, axis=dim)


PERMUTE_GROUP = 8


def shifted(cells, axes, sizes, offsets):
    pairs = []
    places = [()]
    for size in sizes:
        places = [place + (i,) for place in places for i in range(size)]
    for place in places:
        target = tuple((p + o) % n for p, o, n in zip(place, offsets, sizes))
        source_index = 0
        target_index = 0
        for p, q, n in zip(place, target, sizes):
            source_index = source_index * n + p
            target_index = target_index * n + q
        pairs.append((source_index, target_index))
    return lax.ppermute(cells, axes, pairs)


def offset_list(sizes):
    offsets = [()]
    for size in sizes:
        offsets = [offset + (i,) for offset in offsets for i in range(size)]
    return offsets


def chan_halves(cells):
    count = lax.axis_size("chan")
    return [cells] + [
        lax.ppermute(cells, "chan", [(i, (i + shift) % count) for i in range(count)])
        for shift in range(1, count)
    ]


def half_rows(weight, shift, width):
    count = lax.axis_size("chan")
    source = (lax.axis_index("chan") - shift) % count
    return lax.dynamic_slice_in_dim(weight, source * width, width, axis=0)


def split_dot(halves, weight, width):
    total = None
    for shift, half in enumerate(halves):
        term = jnp.dot(half, half_rows(weight, shift, width), preferred_element_type=jnp.float32)
        total = term if total is None else total + term
    return total


def local(
    latent,
    norm1_gain,
    norm1_bias,
    conv_weight,
    conv_bias,
    norm2_gain,
    norm2_bias,
    w_query,
    b_query,
    w_key,
    w_value,
    b_value,
    w_out,
    b_out,
):
    frames, rows_here, columns, channels = latent.shape
    group_size = C // GROUPS
    time_count = lax.axis_size("tm")
    row_count = lax.axis_size("rows")
    chan_count = lax.axis_size("chan")
    time_place = lax.axis_index("tm")
    row_place = lax.axis_index("rows")
    chan_place = lax.axis_index("chan")
    all_rows = rows_here * row_count

    if row_count * time_count <= PERMUTE_GROUP:
        clip = jnp.zeros((time_count * frames, all_rows, columns, channels), latent.dtype)
        for offset in offset_list((row_count, time_count)):
            block = latent if offset == (0, 0) else shifted(
                latent, ("rows", "tm"), (row_count, time_count), offset
            )
            source_row = (row_place - offset[0]) % row_count
            source_time = (time_place - offset[1]) % time_count
            clip = lax.dynamic_update_slice(
                clip, block, (source_time * frames, source_row * rows_here, 0, 0)
            )
    else:
        copies = jnp.broadcast_to(latent[None], (row_count * time_count,) + latent.shape)
        gathered = lax.all_to_all(copies, ("rows", "tm"), 0, 0, tiled=True).reshape(
            (row_count, time_count, frames, rows_here, columns, channels)
        )
        clip = jnp.transpose(gathered, (1, 2, 0, 3, 4, 5)).reshape(
            (time_count * frames, all_rows, columns, channels)
        )

    mean1, var1 = group_stats(clip, group_size, (0, 1, 2, 4))
    frame_index = jnp.clip(
        time_place * frames - 2 + jnp.arange(frames + 2), 0, time_count * frames - 1
    )
    segment = jnp.take(clip, frame_index, axis=0)
    activated = jax.nn.silu(
        apply_norm(segment, mean1, var1, group_size) * norm1_gain + norm1_bias
    ).astype(jnp.bfloat16)
    padded = edge_pad(edge_pad(activated, 1, 1, 1), 2, 1, 1)
    padded_halves = chan_halves(padded)

    block_rows = conv_weight.shape[0]
    start = row_place * block_rows
    first_tap = start // C
    offset = start % C
    span = max(
        (place * block_rows + block_rows - 1) // C - (place * block_rows) // C + 1
        for place in range(row_count)
    )
    out_channels = conv_weight.shape[1]
    placed = lax.dynamic_update_slice(
        jnp.zeros((span * C, out_channels), conv_weight.dtype), conv_weight, (offset, 0)
    ).reshape(span, chan_count, channels, out_channels)
    taps = (block_rows * row_count) // C
    partial = None
    for shift, half in enumerate(padded_halves):
        source = (chan_place - shift) % chan_count
        windows = []
        for step in range(span):
            tap = jnp.minimum(first_tap + step, taps - 1)
            windows.append(
                lax.dynamic_slice(
                    half,
                    (tap // 9, (tap // 3) % 3, tap % 3, 0),
                    (frames, all_rows, columns, channels),
                ).reshape(-1, channels)
            )
        patches = jnp.concatenate(windows, axis=1)
        block = lax.dynamic_index_in_dim(placed, source, axis=1, keepdims=False).reshape(
            span * channels, out_channels
        )
        term = jnp.dot(patches, block, preferred_element_type=jnp.float32)
        partial = term if partial is None else partial + term

    pieces = partial.reshape(frames, row_count, rows_here, columns, out_channels)
    if row_count <= PERMUTE_GROUP:
        convolved = lax.dynamic_index_in_dim(pieces, row_place, axis=1, keepdims=False)
        for shift in range(1, row_count):
            chunk = lax.dynamic_index_in_dim(
                pieces, (row_place + shift) % row_count, axis=1, keepdims=False
            )
            convolved = convolved + shifted(chunk, ("rows",), (row_count,), (shift,))
    else:
        convolved = jnp.sum(lax.all_to_all(pieces, "rows", 1, 1, tiled=True), axis=1)
    own_middle = (latent.astype(jnp.float32) + convolved + conv_bias).astype(jnp.bfloat16)

    if row_count <= PERMUTE_GROUP:
        middle = jnp.zeros((frames, all_rows, columns, out_channels), own_middle.dtype)
        for shift in range(row_count):
            block = own_middle if shift == 0 else shifted(
                own_middle, ("rows",), (row_count,), (shift,)
            )
            source_row = (row_place - shift) % row_count
            middle = lax.dynamic_update_slice(middle, block, (0, source_row * rows_here, 0, 0))
    else:
        middle = lax.all_to_all(
            jnp.tile(own_middle, (1, row_count, 1, 1)), "rows", 1, 1, tiled=True
        )
    mean2, var2 = group_stats(middle, group_size, (1, 2, 4))
    normed = (apply_norm(middle, mean2, var2, group_size) * norm2_gain + norm2_bias).astype(
        jnp.bfloat16
    )
    normed_halves = chan_halves(normed)

    tokens = all_rows * columns
    local_tokens = rows_here * columns
    own_rows = [
        lax.dynamic_slice_in_dim(half, row_place * rows_here, rows_here, axis=1).reshape(
            -1, channels
        )
        for half in normed_halves
    ]
    flat = [half.reshape(-1, channels) for half in normed_halves]
    queries = (
        (split_dot(own_rows, w_query, channels) + b_query)
        .astype(jnp.bfloat16)
        .reshape(frames, local_tokens, C)
    )
    keys = split_dot(flat, w_key, channels).astype(jnp.bfloat16).reshape(frames, tokens, C)
    values = (
        (split_dot(flat, w_value, channels) + b_value)
        .astype(jnp.bfloat16)
        .reshape(frames, tokens, C)
    )
    scores = jnp.einsum("fqc,fkc->fqk", queries, keys, preferred_element_type=jnp.float32) * (
        C ** (-0.5)
    )
    row_peak = jnp.max(scores, axis=2, keepdims=True)
    weights = jnp.exp(scores - row_peak)
    weight_sum = jnp.sum(weights, axis=2, keepdims=True)
    attended = (
        jnp.einsum(
            "fqk,fkc->fqc",
            weights.astype(jnp.bfloat16),
            values,
            preferred_element_type=jnp.float32,
        )
        / weight_sum
    ).astype(jnp.bfloat16)
    out_block = lax.dynamic_slice(w_out, (0, chan_place * out_channels), (C, out_channels))
    out_bias = lax.dynamic_slice(b_out, (chan_place * out_channels,), (out_channels,))
    branch = (
        (jnp.dot(attended.reshape(-1, C), out_block, preferred_element_type=jnp.float32) + out_bias)
        .astype(jnp.bfloat16)
        .reshape(frames, rows_here, columns, out_channels)
    )
    return (own_middle.astype(jnp.float32) + branch.astype(jnp.float32)).astype(jnp.bfloat16)


def solution(mesh):
    in_specs = (
        P(("clips", "tm"), "rows", None, "chan"),
        P("chan"),
        P("chan"),
        P("rows", "chan"),
        P("chan"),
        P("chan"),
        P("chan"),
        P(),
        P(),
        P(),
        P(),
        P(),
        P(),
        P(),
    )
    out_specs = P(("clips", "tm"), "rows", None, "chan")
    return jax.shard_map(local, mesh=mesh, in_specs=in_specs, out_specs=out_specs, check_vma=False)
```

```python
import jax
import jax.numpy as jnp
from jax import lax
from jax.sharding import PartitionSpec as P

C = 512
GROUPS = 32


EPSILON = 1e-06


def group_stats(values, group_size, axes):
    grouped = values.astype(jnp.float32).reshape(
        values.shape[:-1] + (values.shape[-1] // group_size, group_size)
    )
    group_mean = jnp.mean(grouped, axis=axes, keepdims=True)
    centered = grouped - group_mean
    group_var = jnp.mean(centered * centered, axis=axes, keepdims=True)
    return group_mean, group_var


def apply_norm(values, group_mean, group_var, group_size):
    grouped = values.astype(jnp.float32).reshape(
        values.shape[:-1] + (values.shape[-1] // group_size, group_size)
    )
    return ((grouped - group_mean) * lax.rsqrt(group_var + EPSILON)).reshape(values.shape)


def edge_pad(cells, dim, before, after):
    size = cells.shape[dim]
    parts = [lax.slice_in_dim(cells, 0, 1, axis=dim)] * before + [cells]
    parts += [lax.slice_in_dim(cells, size - 1, size, axis=dim)] * after
    return jnp.concatenate(parts, axis=dim)


PERMUTE_GROUP = 8


def shifted(cells, axes, sizes, offsets):
    pairs = []
    places = [()]
    for size in sizes:
        places = [place + (i,) for place in places for i in range(size)]
    for place in places:
        target = tuple((p + o) % n for p, o, n in zip(place, offsets, sizes))
        source_index = 0
        target_index = 0
        for p, q, n in zip(place, target, sizes):
            source_index = source_index * n + p
            target_index = target_index * n + q
        pairs.append((source_index, target_index))
    return lax.ppermute(cells, axes, pairs)


def nearest_first(count):
    order = []
    for step in range(1, count):
        for shift in (step, count - step):
            if 0 < shift < count and shift not in order:
                order.append(shift)
    return order


def chan_halves(cells):
    count = lax.axis_size("chan")
    return [cells] + [
        lax.ppermute(cells, "chan", [(i, (i + shift) % count) for i in range(count)])
        for shift in range(1, count)
    ]


def half_rows(weight, shift, width):
    count = lax.axis_size("chan")
    source = (lax.axis_index("chan") - shift) % count
    return lax.dynamic_slice_in_dim(weight, source * width, width, axis=0)


def split_dot(halves, weight, width):
    total = None
    for shift, half in enumerate(halves):
        term = jnp.dot(half, half_rows(weight, shift, width), preferred_element_type=jnp.float32)
        total = term if total is None else total + term
    return total


def local(
    latent,
    norm1_gain,
    norm1_bias,
    conv_weight,
    conv_bias,
    norm2_gain,
    norm2_bias,
    w_query,
    b_query,
    w_key,
    w_value,
    b_value,
    w_out,
    b_out,
):
    frames, rows_here, columns, channels = latent.shape
    group_size = C // GROUPS
    time_count = lax.axis_size("tm")
    row_count = lax.axis_size("rows")
    chan_count = lax.axis_size("chan")
    time_place = lax.axis_index("tm")
    row_place = lax.axis_index("rows")
    chan_place = lax.axis_index("chan")
    all_rows = rows_here * row_count

    if row_count * time_count <= PERMUTE_GROUP:
        segment_rows = jnp.zeros((frames, all_rows, columns, channels), latent.dtype)
        for shift in [0] + nearest_first(row_count):
            block = latent if shift == 0 else shifted(latent, ("rows",), (row_count,), (shift,))
            source_row = (row_place - shift) % row_count
            segment_rows = lax.dynamic_update_slice(
                segment_rows, block, (0, source_row * rows_here, 0, 0)
            )
        clip = jnp.zeros((time_count * frames, all_rows, columns, channels), latent.dtype)
        for shift in [0] + nearest_first(time_count):
            block = segment_rows if shift == 0 else shifted(
                segment_rows, ("tm",), (time_count,), (shift,)
            )
            source_time = (time_place - shift) % time_count
            clip = lax.dynamic_update_slice(clip, block, (source_time * frames, 0, 0, 0))
    else:
        copies = jnp.broadcast_to(latent[None], (row_count * time_count,) + latent.shape)
        gathered = lax.all_to_all(copies, ("rows", "tm"), 0, 0, tiled=True).reshape(
            (row_count, time_count, frames, rows_here, columns, channels)
        )
        clip = jnp.transpose(gathered, (1, 2, 0, 3, 4, 5)).reshape(
            (time_count * frames, all_rows, columns, channels)
        )

    mean1, var1 = group_stats(clip, group_size, (0, 1, 2, 4))
    frame_index = jnp.clip(
        time_place * frames - 2 + jnp.arange(frames + 2), 0, time_count * frames - 1
    )
    segment = jnp.take(clip, frame_index, axis=0)
    activated = jax.nn.silu(
        apply_norm(segment, mean1, var1, group_size) * norm1_gain + norm1_bias
    ).astype(jnp.bfloat16)
    padded = edge_pad(edge_pad(activated, 1, 1, 1), 2, 1, 1)
    padded_halves = chan_halves(padded)

    block_rows = conv_weight.shape[0]
    start = row_place * block_rows
    first_tap = start // C
    offset = start % C
    span = max(
        (place * block_rows + block_rows - 1) // C - (place * block_rows) // C + 1
        for place in range(row_count)
    )
    out_channels = conv_weight.shape[1]
    placed = lax.dynamic_update_slice(
        jnp.zeros((span * C, out_channels), conv_weight.dtype), conv_weight, (offset, 0)
    ).reshape(span, chan_count, channels, out_channels)
    taps = (block_rows * row_count) // C
    partial = None
    for shift, half in enumerate(padded_halves):
        source = (chan_place - shift) % chan_count
        windows = []
        for step in range(span):
            tap = jnp.minimum(first_tap + step, taps - 1)
            windows.append(
                lax.dynamic_slice(
                    half,
                    (tap // 9, (tap // 3) % 3, tap % 3, 0),
                    (frames, all_rows, columns, channels),
                ).reshape(-1, channels)
            )
        patches = jnp.concatenate(windows, axis=1)
        block = lax.dynamic_index_in_dim(placed, source, axis=1, keepdims=False).reshape(
            span * channels, out_channels
        )
        term = jnp.dot(patches, block, preferred_element_type=jnp.float32)
        partial = term if partial is None else partial + term

    pieces = partial.reshape(frames, row_count, rows_here, columns, out_channels)
    if row_count <= PERMUTE_GROUP:
        convolved = lax.dynamic_index_in_dim(pieces, row_place, axis=1, keepdims=False)
        for shift in nearest_first(row_count):
            chunk = lax.dynamic_index_in_dim(
                pieces, (row_place + shift) % row_count, axis=1, keepdims=False
            )
            convolved = convolved + shifted(chunk, ("rows",), (row_count,), (shift,))
    else:
        convolved = jnp.sum(lax.all_to_all(pieces, "rows", 1, 1, tiled=True), axis=1)
    own_middle = (latent.astype(jnp.float32) + convolved + conv_bias).astype(jnp.bfloat16)

    if row_count <= PERMUTE_GROUP:
        middle = jnp.zeros((frames, all_rows, columns, out_channels), own_middle.dtype)
        for shift in [0] + nearest_first(row_count):
            block = own_middle if shift == 0 else shifted(
                own_middle, ("rows",), (row_count,), (shift,)
            )
            source_row = (row_place - shift) % row_count
            middle = lax.dynamic_update_slice(middle, block, (0, source_row * rows_here, 0, 0))
    else:
        middle = lax.all_to_all(
            jnp.tile(own_middle, (1, row_count, 1, 1)), "rows", 1, 1, tiled=True
        )
    mean2, var2 = group_stats(middle, group_size, (1, 2, 4))
    normed = (apply_norm(middle, mean2, var2, group_size) * norm2_gain + norm2_bias).astype(
        jnp.bfloat16
    )
    normed_halves = chan_halves(normed)

    tokens = all_rows * columns
    local_tokens = rows_here * columns
    own_rows = [
        lax.dynamic_slice_in_dim(half, row_place * rows_here, rows_here, axis=1).reshape(
            -1, channels
        )
        for half in normed_halves
    ]
    flat = [half.reshape(-1, channels) for half in normed_halves]
    queries = (
        (split_dot(own_rows, w_query, channels) + b_query)
        .astype(jnp.bfloat16)
        .reshape(frames, local_tokens, C)
    )
    keys = split_dot(flat, w_key, channels).astype(jnp.bfloat16).reshape(frames, tokens, C)
    values = (
        (split_dot(flat, w_value, channels) + b_value)
        .astype(jnp.bfloat16)
        .reshape(frames, tokens, C)
    )
    scores = jnp.einsum("fqc,fkc->fqk", queries, keys, preferred_element_type=jnp.float32) * (
        C ** (-0.5)
    )
    row_peak = jnp.max(scores, axis=2, keepdims=True)
    weights = jnp.exp(scores - row_peak)
    weight_sum = jnp.sum(weights, axis=2, keepdims=True)
    attended = (
        jnp.einsum(
            "fqk,fkc->fqc",
            weights.astype(jnp.bfloat16),
            values,
            preferred_element_type=jnp.float32,
        )
        / weight_sum
    ).astype(jnp.bfloat16)
    out_block = lax.dynamic_slice(w_out, (0, chan_place * out_channels), (C, out_channels))
    out_bias = lax.dynamic_slice(b_out, (chan_place * out_channels,), (out_channels,))
    branch = (
        (jnp.dot(attended.reshape(-1, C), out_block, preferred_element_type=jnp.float32) + out_bias)
        .astype(jnp.bfloat16)
        .reshape(frames, rows_here, columns, out_channels)
    )
    return (own_middle.astype(jnp.float32) + branch.astype(jnp.float32)).astype(jnp.bfloat16)


def solution(mesh):
    in_specs = (
        P(("clips", "tm"), "rows", None, "chan"),
        P("chan"),
        P("chan"),
        P("rows", "chan"),
        P("chan"),
        P("chan"),
        P("chan"),
        P(),
        P(),
        P(),
        P(),
        P(),
        P(),
        P(),
    )
    out_specs = P(("clips", "tm"), "rows", None, "chan")
    return jax.shard_map(local, mesh=mesh, in_specs=in_specs, out_specs=out_specs, check_vma=False)
```

```python
import jax
import jax.numpy as jnp
from jax import lax
from jax.sharding import PartitionSpec as P

C = 512
GROUPS = 32


EPSILON = 1e-06


def group_stats(values, group_size, axes):
    grouped = values.astype(jnp.float32).reshape(
        values.shape[:-1] + (values.shape[-1] // group_size, group_size)
    )
    group_mean = jnp.mean(grouped, axis=axes, keepdims=True)
    centered = grouped - group_mean
    group_var = jnp.mean(centered * centered, axis=axes, keepdims=True)
    return group_mean, group_var


def apply_norm(values, group_mean, group_var, group_size):
    grouped = values.astype(jnp.float32).reshape(
        values.shape[:-1] + (values.shape[-1] // group_size, group_size)
    )
    return ((grouped - group_mean) * lax.rsqrt(group_var + EPSILON)).reshape(values.shape)


def edge_pad(cells, dim, before, after):
    size = cells.shape[dim]
    parts = [lax.slice_in_dim(cells, 0, 1, axis=dim)] * before + [cells]
    parts += [lax.slice_in_dim(cells, size - 1, size, axis=dim)] * after
    return jnp.concatenate(parts, axis=dim)


PERMUTE_GROUP = 8


def shifted(cells, axes, sizes, offsets):
    pairs = []
    places = [()]
    for size in sizes:
        places = [place + (i,) for place in places for i in range(size)]
    for place in places:
        target = tuple((p + o) % n for p, o, n in zip(place, offsets, sizes))
        source_index = 0
        target_index = 0
        for p, q, n in zip(place, target, sizes):
            source_index = source_index * n + p
            target_index = target_index * n + q
        pairs.append((source_index, target_index))
    return lax.ppermute(cells, axes, pairs)


def nearest_first(count):
    order = []
    for step in range(1, count):
        for shift in (step, count - step):
            if 0 < shift < count and shift not in order:
                order.append(shift)
    return order


def chan_halves(cells):
    count = lax.axis_size("chan")
    return [cells] + [
        lax.ppermute(cells, "chan", [(i, (i + shift) % count) for i in range(count)])
        for shift in range(1, count)
    ]


def half_rows(weight, shift, width):
    count = lax.axis_size("chan")
    source = (lax.axis_index("chan") - shift) % count
    return lax.dynamic_slice_in_dim(weight, source * width, width, axis=0)


def split_dot(halves, weight, width):
    total = None
    for shift, half in enumerate(halves):
        term = jnp.dot(half, half_rows(weight, shift, width), preferred_element_type=jnp.float32)
        total = term if total is None else total + term
    return total


def local(
    latent,
    norm1_gain,
    norm1_bias,
    conv_weight,
    conv_bias,
    norm2_gain,
    norm2_bias,
    w_query,
    b_query,
    w_key,
    w_value,
    b_value,
    w_out,
    b_out,
):
    frames, rows_here, columns, channels = latent.shape
    group_size = C // GROUPS
    time_count = lax.axis_size("tm")
    row_count = lax.axis_size("rows")
    chan_count = lax.axis_size("chan")
    time_place = lax.axis_index("tm")
    row_place = lax.axis_index("rows")
    chan_place = lax.axis_index("chan")
    all_rows = rows_here * row_count

    if row_count * time_count <= PERMUTE_GROUP:
        segment_rows = jnp.zeros((frames, all_rows, columns, channels), latent.dtype)
        for shift in [0] + nearest_first(row_count):
            block = latent if shift == 0 else shifted(latent, ("rows",), (row_count,), (shift,))
            source_row = (row_place - shift) % row_count
            segment_rows = lax.dynamic_update_slice(
                segment_rows, block, (0, source_row * rows_here, 0, 0)
            )
        clip = jnp.zeros((time_count * frames, all_rows, columns, channels), latent.dtype)
        for shift in [0] + nearest_first(time_count):
            block = segment_rows if shift == 0 else shifted(
                segment_rows, ("tm",), (time_count,), (shift,)
            )
            source_time = (time_place - shift) % time_count
            clip = lax.dynamic_update_slice(clip, block, (source_time * frames, 0, 0, 0))
    else:
        copies = jnp.broadcast_to(latent[None], (row_count * time_count,) + latent.shape)
        gathered = lax.all_to_all(copies, ("rows", "tm"), 0, 0, tiled=True).reshape(
            (row_count, time_count, frames, rows_here, columns, channels)
        )
        clip = jnp.transpose(gathered, (1, 2, 0, 3, 4, 5)).reshape(
            (time_count * frames, all_rows, columns, channels)
        )

    mean1, var1 = group_stats(clip, group_size, (0, 1, 2, 4))
    frame_index = jnp.clip(
        time_place * frames - 2 + jnp.arange(frames + 2), 0, time_count * frames - 1
    )
    segment = jnp.take(clip, frame_index, axis=0)
    activated = jax.nn.silu(
        apply_norm(segment, mean1, var1, group_size) * norm1_gain + norm1_bias
    ).astype(jnp.bfloat16)
    padded = edge_pad(edge_pad(activated, 1, 1, 1), 2, 1, 1)
    padded_halves = chan_halves(padded)

    block_rows = conv_weight.shape[0]
    start = row_place * block_rows
    first_tap = start // C
    offset = start % C
    span = max(
        (place * block_rows + block_rows - 1) // C - (place * block_rows) // C + 1
        for place in range(row_count)
    )
    out_channels = conv_weight.shape[1]
    placed = lax.dynamic_update_slice(
        jnp.zeros((span * C, out_channels), conv_weight.dtype), conv_weight, (offset, 0)
    ).reshape(span, chan_count, channels, out_channels)
    taps = (block_rows * row_count) // C
    blocks = [
        lax.dynamic_index_in_dim(
            placed, (chan_place - shift) % chan_count, axis=1, keepdims=False
        ).reshape(span * channels, out_channels)
        for shift in range(chan_count)
    ]

    def row_partial(row_block):
        total = None
        for half, block in zip(padded_halves, blocks):
            windows = []
            for step in range(span):
                tap = jnp.minimum(first_tap + step, taps - 1)
                windows.append(
                    lax.dynamic_slice(
                        half,
                        (tap // 9, (tap // 3) % 3 + row_block * rows_here, tap % 3, 0),
                        (frames, rows_here, columns, channels),
                    ).reshape(-1, channels)
                )
            term = jnp.dot(
                jnp.concatenate(windows, axis=1), block, preferred_element_type=jnp.float32
            )
            total = term if total is None else total + term
        return total.reshape(frames, rows_here, columns, out_channels)

    if row_count <= PERMUTE_GROUP:
        received = []
        for shift in nearest_first(row_count):
            chunk = row_partial((row_place + shift) % row_count)
            received.append(shifted(chunk, ("rows",), (row_count,), (shift,)))
        convolved = row_partial(row_place)
        for piece in received:
            convolved = convolved + piece
    else:
        pieces = jnp.stack([row_partial(block) for block in range(row_count)], axis=1)
        convolved = jnp.sum(lax.all_to_all(pieces, "rows", 1, 1, tiled=True), axis=1)
    own_middle = (latent.astype(jnp.float32) + convolved + conv_bias).astype(jnp.bfloat16)

    if row_count <= PERMUTE_GROUP:
        middle = jnp.zeros((frames, all_rows, columns, out_channels), own_middle.dtype)
        for shift in [0] + nearest_first(row_count):
            block = own_middle if shift == 0 else shifted(
                own_middle, ("rows",), (row_count,), (shift,)
            )
            source_row = (row_place - shift) % row_count
            middle = lax.dynamic_update_slice(middle, block, (0, source_row * rows_here, 0, 0))
    else:
        middle = lax.all_to_all(
            jnp.tile(own_middle, (1, row_count, 1, 1)), "rows", 1, 1, tiled=True
        )
    mean2, var2 = group_stats(middle, group_size, (1, 2, 4))
    normed = (apply_norm(middle, mean2, var2, group_size) * norm2_gain + norm2_bias).astype(
        jnp.bfloat16
    )
    normed_halves = chan_halves(normed)

    tokens = all_rows * columns
    local_tokens = rows_here * columns
    own_rows = [
        lax.dynamic_slice_in_dim(half, row_place * rows_here, rows_here, axis=1).reshape(
            -1, channels
        )
        for half in normed_halves
    ]
    flat = [half.reshape(-1, channels) for half in normed_halves]
    queries = (
        (split_dot(own_rows, w_query, channels) + b_query)
        .astype(jnp.bfloat16)
        .reshape(frames, local_tokens, C)
    )
    keys = split_dot(flat, w_key, channels).astype(jnp.bfloat16).reshape(frames, tokens, C)
    values = (
        (split_dot(flat, w_value, channels) + b_value)
        .astype(jnp.bfloat16)
        .reshape(frames, tokens, C)
    )
    scores = jnp.einsum("fqc,fkc->fqk", queries, keys, preferred_element_type=jnp.float32) * (
        C ** (-0.5)
    )
    row_peak = jnp.max(scores, axis=2, keepdims=True)
    weights = jnp.exp(scores - row_peak)
    weight_sum = jnp.sum(weights, axis=2, keepdims=True)
    attended = (
        jnp.einsum(
            "fqk,fkc->fqc",
            weights.astype(jnp.bfloat16),
            values,
            preferred_element_type=jnp.float32,
        )
        / weight_sum
    ).astype(jnp.bfloat16)
    out_block = lax.dynamic_slice(w_out, (0, chan_place * out_channels), (C, out_channels))
    out_bias = lax.dynamic_slice(b_out, (chan_place * out_channels,), (out_channels,))
    branch = (
        (jnp.dot(attended.reshape(-1, C), out_block, preferred_element_type=jnp.float32) + out_bias)
        .astype(jnp.bfloat16)
        .reshape(frames, rows_here, columns, out_channels)
    )
    return (own_middle.astype(jnp.float32) + branch.astype(jnp.float32)).astype(jnp.bfloat16)


def solution(mesh):
    in_specs = (
        P(("clips", "tm"), "rows", None, "chan"),
        P("chan"),
        P("chan"),
        P("rows", "chan"),
        P("chan"),
        P("chan"),
        P("chan"),
        P(),
        P(),
        P(),
        P(),
        P(),
        P(),
        P(),
    )
    out_specs = P(("clips", "tm"), "rows", None, "chan")
    return jax.shard_map(local, mesh=mesh, in_specs=in_specs, out_specs=out_specs, check_vma=False)
```

```python
import jax
import jax.numpy as jnp
from jax import lax
from jax.experimental import pallas as pl
from jax.experimental.pallas import tpu as pltpu
from jax.sharding import PartitionSpec as P

C = 512
GROUPS = 32


EPSILON = 1e-06


def group_stats(values, group_size, axes):
    grouped = values.astype(jnp.float32).reshape(
        values.shape[:-1] + (values.shape[-1] // group_size, group_size)
    )
    group_mean = jnp.mean(grouped, axis=axes, keepdims=True)
    centered = grouped - group_mean
    group_var = jnp.mean(centered * centered, axis=axes, keepdims=True)
    return group_mean, group_var


def apply_norm(values, group_mean, group_var, group_size):
    grouped = values.astype(jnp.float32).reshape(
        values.shape[:-1] + (values.shape[-1] // group_size, group_size)
    )
    return ((grouped - group_mean) * lax.rsqrt(group_var + EPSILON)).reshape(values.shape)


def edge_pad(cells, dim, before, after):
    size = cells.shape[dim]
    parts = [lax.slice_in_dim(cells, 0, 1, axis=dim)] * before + [cells]
    parts += [lax.slice_in_dim(cells, size - 1, size, axis=dim)] * after
    return jnp.concatenate(parts, axis=dim)


def conv_taps_kernel(taps_ref, shifted_ref, weight_ref, init_ref, out_ref):
    _, frames, rows, columns, channels = shifted_ref.shape
    frames, rows = frames - 2, rows - 2
    total = init_ref[...]
    for step in range(weight_ref.shape[0]):
        window = shifted_ref[
            taps_ref[step, 2], pl.ds(taps_ref[step, 0], frames), pl.ds(taps_ref[step, 1], rows)
        ]
        total = total + jnp.dot(
            window.reshape(frames * rows * columns, channels),
            weight_ref[step],
            preferred_element_type=jnp.float32,
        )
    out_ref[...] = total


def conv_taps(taps, padded, weight, init):
    columns = padded.shape[2] - 2
    shifted = jnp.stack([padded[:, :, e : e + columns] for e in range(3)])
    return pl.pallas_call(
        conv_taps_kernel,
        out_shape=jax.ShapeDtypeStruct(init.shape, jnp.float32),
        in_specs=[
            pl.BlockSpec(memory_space=pltpu.SMEM),
            pl.BlockSpec(memory_space=pltpu.VMEM),
            pl.BlockSpec(memory_space=pltpu.VMEM),
            pl.BlockSpec(memory_space=pltpu.VMEM),
        ],
        out_specs=pl.BlockSpec(memory_space=pltpu.VMEM),
    )(taps, shifted, weight, init)


PERMUTE_GROUP = 8


def shifted(cells, axes, sizes, offsets):
    pairs = []
    places = [()]
    for size in sizes:
        places = [place + (i,) for place in places for i in range(size)]
    for place in places:
        target = tuple((p + o) % n for p, o, n in zip(place, offsets, sizes))
        source_index = 0
        target_index = 0
        for p, q, n in zip(place, target, sizes):
            source_index = source_index * n + p
            target_index = target_index * n + q
        pairs.append((source_index, target_index))
    return lax.ppermute(cells, axes, pairs)


def nearest_first(count):
    order = []
    for step in range(1, count):
        for shift in (step, count - step):
            if 0 < shift < count and shift not in order:
                order.append(shift)
    return order


def chan_halves(cells):
    count = lax.axis_size("chan")
    return [cells] + [
        lax.ppermute(cells, "chan", [(i, (i + shift) % count) for i in range(count)])
        for shift in range(1, count)
    ]


def half_rows(weight, shift, width):
    count = lax.axis_size("chan")
    source = (lax.axis_index("chan") - shift) % count
    return lax.dynamic_slice_in_dim(weight, source * width, width, axis=0)


def split_dot(halves, weight, width):
    total = None
    for shift, half in enumerate(halves):
        term = jnp.dot(half, half_rows(weight, shift, width), preferred_element_type=jnp.float32)
        total = term if total is None else total + term
    return total


def local(
    latent,
    norm1_gain,
    norm1_bias,
    conv_weight,
    conv_bias,
    norm2_gain,
    norm2_bias,
    w_query,
    b_query,
    w_key,
    w_value,
    b_value,
    w_out,
    b_out,
):
    frames, rows_here, columns, channels = latent.shape
    group_size = C // GROUPS
    time_count = lax.axis_size("tm")
    row_count = lax.axis_size("rows")
    chan_count = lax.axis_size("chan")
    time_place = lax.axis_index("tm")
    row_place = lax.axis_index("rows")
    chan_place = lax.axis_index("chan")
    all_rows = rows_here * row_count

    if row_count * time_count <= PERMUTE_GROUP:
        segment_rows = jnp.zeros((frames, all_rows, columns, channels), latent.dtype)
        for shift in [0] + nearest_first(row_count):
            block = latent if shift == 0 else shifted(latent, ("rows",), (row_count,), (shift,))
            source_row = (row_place - shift) % row_count
            segment_rows = lax.dynamic_update_slice(
                segment_rows, block, (0, source_row * rows_here, 0, 0)
            )
        clip = jnp.zeros((time_count * frames, all_rows, columns, channels), latent.dtype)
        for shift in [0] + nearest_first(time_count):
            block = segment_rows if shift == 0 else shifted(
                segment_rows, ("tm",), (time_count,), (shift,)
            )
            source_time = (time_place - shift) % time_count
            clip = lax.dynamic_update_slice(clip, block, (source_time * frames, 0, 0, 0))
    else:
        copies = jnp.broadcast_to(latent[None], (row_count * time_count,) + latent.shape)
        gathered = lax.all_to_all(copies, ("rows", "tm"), 0, 0, tiled=True).reshape(
            (row_count, time_count, frames, rows_here, columns, channels)
        )
        clip = jnp.transpose(gathered, (1, 2, 0, 3, 4, 5)).reshape(
            (time_count * frames, all_rows, columns, channels)
        )

    mean1, var1 = group_stats(clip, group_size, (0, 1, 2, 4))
    frame_index = jnp.clip(
        time_place * frames - 2 + jnp.arange(frames + 2), 0, time_count * frames - 1
    )
    segment = jnp.take(clip, frame_index, axis=0)
    activated = jax.nn.silu(
        apply_norm(segment, mean1, var1, group_size) * norm1_gain + norm1_bias
    ).astype(jnp.bfloat16)
    padded = edge_pad(edge_pad(activated, 1, 1, 1), 2, 1, 1)
    padded_halves = chan_halves(padded)

    block_rows = conv_weight.shape[0]
    start = row_place * block_rows
    first_tap = start // C
    offset = start % C
    span = max(
        (place * block_rows + block_rows - 1) // C - (place * block_rows) // C + 1
        for place in range(row_count)
    )
    out_channels = conv_weight.shape[1]
    placed = lax.dynamic_update_slice(
        jnp.zeros((span * C, out_channels), conv_weight.dtype), conv_weight, (offset, 0)
    ).reshape(span, chan_count, channels, out_channels)
    taps = (block_rows * row_count) // C
    if all_rows * columns * frames <= 1024:
        steps = jnp.minimum(first_tap + jnp.arange(span), taps - 1)
        tap_table = jnp.stack([steps // 9, (steps // 3) % 3, steps % 3], axis=1).astype(jnp.int32)
        partial = jnp.zeros((frames * all_rows * columns, out_channels), jnp.float32)
        for shift, half in enumerate(padded_halves):
            source = (chan_place - shift) % chan_count
            block = lax.dynamic_index_in_dim(placed, source, axis=1, keepdims=False)
            partial = conv_taps(tap_table, half, block, partial)
    else:
        partial = None
        for shift, half in enumerate(padded_halves):
            source = (chan_place - shift) % chan_count
            windows = []
            for step in range(span):
                tap = jnp.minimum(first_tap + step, taps - 1)
                windows.append(
                    lax.dynamic_slice(
                        half,
                        (tap // 9, (tap // 3) % 3, tap % 3, 0),
                        (frames, all_rows, columns, channels),
                    ).reshape(-1, channels)
                )
            patches = jnp.concatenate(windows, axis=1)
            block = lax.dynamic_index_in_dim(placed, source, axis=1, keepdims=False).reshape(
                span * channels, out_channels
            )
            term = jnp.dot(patches, block, preferred_element_type=jnp.float32)
            partial = term if partial is None else partial + term

    pieces = partial.reshape(frames, row_count, rows_here, columns, out_channels)
    if row_count <= PERMUTE_GROUP:
        convolved = lax.dynamic_index_in_dim(pieces, row_place, axis=1, keepdims=False)
        for shift in nearest_first(row_count):
            chunk = lax.dynamic_index_in_dim(
                pieces, (row_place + shift) % row_count, axis=1, keepdims=False
            )
            convolved = convolved + shifted(chunk, ("rows",), (row_count,), (shift,))
    else:
        convolved = jnp.sum(lax.all_to_all(pieces, "rows", 1, 1, tiled=True), axis=1)
    own_middle = (latent.astype(jnp.float32) + convolved + conv_bias).astype(jnp.bfloat16)

    if row_count <= PERMUTE_GROUP:
        middle = jnp.zeros((frames, all_rows, columns, out_channels), own_middle.dtype)
        for shift in [0] + nearest_first(row_count):
            block = own_middle if shift == 0 else shifted(
                own_middle, ("rows",), (row_count,), (shift,)
            )
            source_row = (row_place - shift) % row_count
            middle = lax.dynamic_update_slice(middle, block, (0, source_row * rows_here, 0, 0))
    else:
        middle = lax.all_to_all(
            jnp.tile(own_middle, (1, row_count, 1, 1)), "rows", 1, 1, tiled=True
        )
    mean2, var2 = group_stats(middle, group_size, (1, 2, 4))
    normed = (apply_norm(middle, mean2, var2, group_size) * norm2_gain + norm2_bias).astype(
        jnp.bfloat16
    )
    normed_halves = chan_halves(normed)

    tokens = all_rows * columns
    local_tokens = rows_here * columns
    own_rows = [
        lax.dynamic_slice_in_dim(half, row_place * rows_here, rows_here, axis=1).reshape(
            -1, channels
        )
        for half in normed_halves
    ]
    flat = [half.reshape(-1, channels) for half in normed_halves]
    queries = (
        (split_dot(own_rows, w_query, channels) + b_query)
        .astype(jnp.bfloat16)
        .reshape(frames, local_tokens, C)
    )
    keys = split_dot(flat, w_key, channels).astype(jnp.bfloat16).reshape(frames, tokens, C)
    values = (
        (split_dot(flat, w_value, channels) + b_value)
        .astype(jnp.bfloat16)
        .reshape(frames, tokens, C)
    )
    scores = jnp.einsum("fqc,fkc->fqk", queries, keys, preferred_element_type=jnp.float32) * (
        C ** (-0.5)
    )
    row_peak = jnp.max(scores, axis=2, keepdims=True)
    weights = jnp.exp(scores - row_peak)
    weight_sum = jnp.sum(weights, axis=2, keepdims=True)
    attended = (
        jnp.einsum(
            "fqk,fkc->fqc",
            weights.astype(jnp.bfloat16),
            values,
            preferred_element_type=jnp.float32,
        )
        / weight_sum
    ).astype(jnp.bfloat16)
    out_block = lax.dynamic_slice(w_out, (0, chan_place * out_channels), (C, out_channels))
    out_bias = lax.dynamic_slice(b_out, (chan_place * out_channels,), (out_channels,))
    branch = (
        (jnp.dot(attended.reshape(-1, C), out_block, preferred_element_type=jnp.float32) + out_bias)
        .astype(jnp.bfloat16)
        .reshape(frames, rows_here, columns, out_channels)
    )
    return (own_middle.astype(jnp.float32) + branch.astype(jnp.float32)).astype(jnp.bfloat16)


def solution(mesh):
    in_specs = (
        P(("clips", "tm"), "rows", None, "chan"),
        P("chan"),
        P("chan"),
        P("rows", "chan"),
        P("chan"),
        P("chan"),
        P("chan"),
        P(),
        P(),
        P(),
        P(),
        P(),
        P(),
        P(),
    )
    out_specs = P(("clips", "tm"), "rows", None, "chan")
    return jax.shard_map(local, mesh=mesh, in_specs=in_specs, out_specs=out_specs, check_vma=False)
```

```python
import jax
import jax.numpy as jnp
from jax import lax
from jax.sharding import PartitionSpec as P

C = 512
GROUPS = 32


EPSILON = 1e-06


def group_stats(values, group_size, axes):
    grouped = values.astype(jnp.float32).reshape(
        values.shape[:-1] + (values.shape[-1] // group_size, group_size)
    )
    group_mean = jnp.mean(grouped, axis=axes, keepdims=True)
    centered = grouped - group_mean
    group_var = jnp.mean(centered * centered, axis=axes, keepdims=True)
    return group_mean, group_var


def apply_norm(values, group_mean, group_var, group_size):
    grouped = values.astype(jnp.float32).reshape(
        values.shape[:-1] + (values.shape[-1] // group_size, group_size)
    )
    return ((grouped - group_mean) * lax.rsqrt(group_var + EPSILON)).reshape(values.shape)


def edge_pad(cells, dim, before, after):
    size = cells.shape[dim]
    parts = [lax.slice_in_dim(cells, 0, 1, axis=dim)] * before + [cells]
    parts += [lax.slice_in_dim(cells, size - 1, size, axis=dim)] * after
    return jnp.concatenate(parts, axis=dim)


PERMUTE_GROUP = 8


def shifted(cells, axes, sizes, offsets):
    pairs = []
    places = [()]
    for size in sizes:
        places = [place + (i,) for place in places for i in range(size)]
    for place in places:
        target = tuple((p + o) % n for p, o, n in zip(place, offsets, sizes))
        source_index = 0
        target_index = 0
        for p, q, n in zip(place, target, sizes):
            source_index = source_index * n + p
            target_index = target_index * n + q
        pairs.append((source_index, target_index))
    return lax.ppermute(cells, axes, pairs)


def nearest_first(count):
    order = []
    for step in range(1, count):
        for shift in (step, count - step):
            if 0 < shift < count and shift not in order:
                order.append(shift)
    return order


def chan_halves(cells):
    count = lax.axis_size("chan")
    return [cells] + [
        lax.ppermute(cells, "chan", [(i, (i + shift) % count) for i in range(count)])
        for shift in range(1, count)
    ]


def half_rows(weight, shift, width):
    count = lax.axis_size("chan")
    source = (lax.axis_index("chan") - shift) % count
    return lax.dynamic_slice_in_dim(weight, source * width, width, axis=0)


def split_dot(halves, weight, width):
    total = None
    for shift, half in enumerate(halves):
        term = jnp.dot(half, half_rows(weight, shift, width), preferred_element_type=jnp.float32)
        total = term if total is None else total + term
    return total


def local(
    latent,
    norm1_gain,
    norm1_bias,
    conv_weight,
    conv_bias,
    norm2_gain,
    norm2_bias,
    w_query,
    b_query,
    w_key,
    w_value,
    b_value,
    w_out,
    b_out,
):
    frames, rows_here, columns, channels = latent.shape
    group_size = C // GROUPS
    time_count = lax.axis_size("tm")
    row_count = lax.axis_size("rows")
    chan_count = lax.axis_size("chan")
    time_place = lax.axis_index("tm")
    row_place = lax.axis_index("rows")
    chan_place = lax.axis_index("chan")
    all_rows = rows_here * row_count

    if row_count * time_count <= PERMUTE_GROUP:
        segment_rows = jnp.zeros((frames, all_rows, columns, channels), latent.dtype)
        for shift in [0] + nearest_first(row_count):
            block = latent if shift == 0 else shifted(latent, ("rows",), (row_count,), (shift,))
            source_row = (row_place - shift) % row_count
            segment_rows = lax.dynamic_update_slice(
                segment_rows, block, (0, source_row * rows_here, 0, 0)
            )
        clip = jnp.zeros((time_count * frames, all_rows, columns, channels), latent.dtype)
        for shift in [0] + nearest_first(time_count):
            block = segment_rows if shift == 0 else shifted(
                segment_rows, ("tm",), (time_count,), (shift,)
            )
            source_time = (time_place - shift) % time_count
            clip = lax.dynamic_update_slice(clip, block, (source_time * frames, 0, 0, 0))
    else:
        copies = jnp.broadcast_to(latent[None], (row_count * time_count,) + latent.shape)
        gathered = lax.all_to_all(copies, ("rows", "tm"), 0, 0, tiled=True).reshape(
            (row_count, time_count, frames, rows_here, columns, channels)
        )
        clip = jnp.transpose(gathered, (1, 2, 0, 3, 4, 5)).reshape(
            (time_count * frames, all_rows, columns, channels)
        )

    mean1, var1 = group_stats(clip, group_size, (0, 1, 2, 4))
    frame_index = jnp.clip(
        time_place * frames - 2 + jnp.arange(frames + 2), 0, time_count * frames - 1
    )
    segment = jnp.take(clip, frame_index, axis=0)
    activated = jax.nn.silu(
        apply_norm(segment, mean1, var1, group_size) * norm1_gain + norm1_bias
    ).astype(jnp.bfloat16)
    padded_halves = [
        edge_pad(edge_pad(half, 1, 1, 1), 2, 1, 1) for half in chan_halves(activated)
    ]

    block_rows = conv_weight.shape[0]
    start = row_place * block_rows
    first_tap = start // C
    offset = start % C
    span = max(
        (place * block_rows + block_rows - 1) // C - (place * block_rows) // C + 1
        for place in range(row_count)
    )
    out_channels = conv_weight.shape[1]
    placed = lax.dynamic_update_slice(
        jnp.zeros((span * C, out_channels), conv_weight.dtype), conv_weight, (offset, 0)
    ).reshape(span, chan_count, channels, out_channels)
    taps = (block_rows * row_count) // C
    partial = None
    for shift, half in enumerate(padded_halves):
        source = (chan_place - shift) % chan_count
        windows = []
        for step in range(span):
            tap = jnp.minimum(first_tap + step, taps - 1)
            windows.append(
                lax.dynamic_slice(
                    half,
                    (tap // 9, (tap // 3) % 3, tap % 3, 0),
                    (frames, all_rows, columns, channels),
                ).reshape(-1, channels)
            )
        patches = jnp.concatenate(windows, axis=1)
        block = lax.dynamic_index_in_dim(placed, source, axis=1, keepdims=False).reshape(
            span * channels, out_channels
        )
        term = jnp.dot(patches, block, preferred_element_type=jnp.float32)
        partial = term if partial is None else partial + term

    pieces = partial.reshape(frames, row_count, rows_here, columns, out_channels)
    if row_count <= PERMUTE_GROUP:
        convolved = lax.dynamic_index_in_dim(pieces, row_place, axis=1, keepdims=False)
        for shift in nearest_first(row_count):
            chunk = lax.dynamic_index_in_dim(
                pieces, (row_place + shift) % row_count, axis=1, keepdims=False
            )
            convolved = convolved + shifted(chunk, ("rows",), (row_count,), (shift,))
    else:
        convolved = jnp.sum(lax.all_to_all(pieces, "rows", 1, 1, tiled=True), axis=1)
    own_middle = (latent.astype(jnp.float32) + convolved + conv_bias).astype(jnp.bfloat16)

    if row_count <= PERMUTE_GROUP:
        middle = jnp.zeros((frames, all_rows, columns, out_channels), own_middle.dtype)
        for shift in [0] + nearest_first(row_count):
            block = own_middle if shift == 0 else shifted(
                own_middle, ("rows",), (row_count,), (shift,)
            )
            source_row = (row_place - shift) % row_count
            middle = lax.dynamic_update_slice(middle, block, (0, source_row * rows_here, 0, 0))
    else:
        middle = lax.all_to_all(
            jnp.tile(own_middle, (1, row_count, 1, 1)), "rows", 1, 1, tiled=True
        )
    mean2, var2 = group_stats(middle, group_size, (1, 2, 4))
    normed = (apply_norm(middle, mean2, var2, group_size) * norm2_gain + norm2_bias).astype(
        jnp.bfloat16
    )
    normed_halves = chan_halves(normed)

    tokens = all_rows * columns
    local_tokens = rows_here * columns
    own_rows = [
        lax.dynamic_slice_in_dim(half, row_place * rows_here, rows_here, axis=1).reshape(
            -1, channels
        )
        for half in normed_halves
    ]
    flat = [half.reshape(-1, channels) for half in normed_halves]
    queries = (
        (split_dot(own_rows, w_query, channels) + b_query)
        .astype(jnp.bfloat16)
        .reshape(frames, local_tokens, C)
    )
    keys = split_dot(flat, w_key, channels).astype(jnp.bfloat16).reshape(frames, tokens, C)
    values = (
        (split_dot(flat, w_value, channels) + b_value)
        .astype(jnp.bfloat16)
        .reshape(frames, tokens, C)
    )
    scores = jnp.einsum("fqc,fkc->fqk", queries, keys, preferred_element_type=jnp.float32) * (
        C ** (-0.5)
    )
    row_peak = jnp.max(scores, axis=2, keepdims=True)
    weights = jnp.exp(scores - row_peak)
    weight_sum = jnp.sum(weights, axis=2, keepdims=True)
    attended = (
        jnp.einsum(
            "fqk,fkc->fqc",
            weights.astype(jnp.bfloat16),
            values,
            preferred_element_type=jnp.float32,
        )
        / weight_sum
    ).astype(jnp.bfloat16)
    out_block = lax.dynamic_slice(w_out, (0, chan_place * out_channels), (C, out_channels))
    out_bias = lax.dynamic_slice(b_out, (chan_place * out_channels,), (out_channels,))
    branch = (
        (jnp.dot(attended.reshape(-1, C), out_block, preferred_element_type=jnp.float32) + out_bias)
        .astype(jnp.bfloat16)
        .reshape(frames, rows_here, columns, out_channels)
    )
    return (own_middle.astype(jnp.float32) + branch.astype(jnp.float32)).astype(jnp.bfloat16)


def solution(mesh):
    in_specs = (
        P(("clips", "tm"), "rows", None, "chan"),
        P("chan"),
        P("chan"),
        P("rows", "chan"),
        P("chan"),
        P("chan"),
        P("chan"),
        P(),
        P(),
        P(),
        P(),
        P(),
        P(),
        P(),
    )
    out_specs = P(("clips", "tm"), "rows", None, "chan")
    return jax.shard_map(local, mesh=mesh, in_specs=in_specs, out_specs=out_specs, check_vma=False)
```

```python
import jax
import jax.numpy as jnp
from jax import lax
from jax.sharding import PartitionSpec as P

C = 512
GROUPS = 32


EPSILON = 1e-06


def group_stats(values, group_size, axes):
    grouped = values.astype(jnp.float32).reshape(
        values.shape[:-1] + (values.shape[-1] // group_size, group_size)
    )
    group_mean = jnp.mean(grouped, axis=axes, keepdims=True)
    centered = grouped - group_mean
    group_var = jnp.mean(centered * centered, axis=axes, keepdims=True)
    return group_mean, group_var


def merged_stats(first, second):
    (mean_a, var_a), (mean_b, var_b) = first, second
    delta = mean_b - mean_a
    return mean_a + 0.5 * delta, 0.5 * (var_a + var_b) + 0.25 * delta * delta


def apply_norm(values, group_mean, group_var, group_size):
    grouped = values.astype(jnp.float32).reshape(
        values.shape[:-1] + (values.shape[-1] // group_size, group_size)
    )
    return ((grouped - group_mean) * lax.rsqrt(group_var + EPSILON)).reshape(values.shape)


def edge_pad(cells, dim, before, after):
    size = cells.shape[dim]
    parts = [lax.slice_in_dim(cells, 0, 1, axis=dim)] * before + [cells]
    parts += [lax.slice_in_dim(cells, size - 1, size, axis=dim)] * after
    return jnp.concatenate(parts, axis=dim)


PERMUTE_GROUP = 8


def shifted(cells, axes, sizes, offsets):
    pairs = []
    places = [()]
    for size in sizes:
        places = [place + (i,) for place in places for i in range(size)]
    for place in places:
        target = tuple((p + o) % n for p, o, n in zip(place, offsets, sizes))
        source_index = 0
        target_index = 0
        for p, q, n in zip(place, target, sizes):
            source_index = source_index * n + p
            target_index = target_index * n + q
        pairs.append((source_index, target_index))
    return lax.ppermute(cells, axes, pairs)


def nearest_first(count):
    order = []
    for step in range(1, count):
        for shift in (step, count - step):
            if 0 < shift < count and shift not in order:
                order.append(shift)
    return order


def chan_halves(cells):
    count = lax.axis_size("chan")
    return [cells] + [
        lax.ppermute(cells, "chan", [(i, (i + shift) % count) for i in range(count)])
        for shift in range(1, count)
    ]


def half_rows(weight, shift, width):
    count = lax.axis_size("chan")
    source = (lax.axis_index("chan") - shift) % count
    return lax.dynamic_slice_in_dim(weight, source * width, width, axis=0)


def split_dot(halves, weight, width):
    total = None
    for shift, half in enumerate(halves):
        term = jnp.dot(half, half_rows(weight, shift, width), preferred_element_type=jnp.float32)
        total = term if total is None else total + term
    return total


def local(
    latent,
    norm1_gain,
    norm1_bias,
    conv_weight,
    conv_bias,
    norm2_gain,
    norm2_bias,
    w_query,
    b_query,
    w_key,
    w_value,
    b_value,
    w_out,
    b_out,
):
    frames, rows_here, columns, channels = latent.shape
    group_size = C // GROUPS
    time_count = lax.axis_size("tm")
    row_count = lax.axis_size("rows")
    chan_count = lax.axis_size("chan")
    time_place = lax.axis_index("tm")
    row_place = lax.axis_index("rows")
    chan_place = lax.axis_index("chan")
    all_rows = rows_here * row_count

    if row_count * time_count <= PERMUTE_GROUP:
        segment_rows = jnp.zeros((frames, all_rows, columns, channels), latent.dtype)
        for shift in [0] + nearest_first(row_count):
            block = latent if shift == 0 else shifted(latent, ("rows",), (row_count,), (shift,))
            source_row = (row_place - shift) % row_count
            segment_rows = lax.dynamic_update_slice(
                segment_rows, block, (0, source_row * rows_here, 0, 0)
            )
        clip = jnp.zeros((time_count * frames, all_rows, columns, channels), latent.dtype)
        block_stats = []
        for shift in [0] + nearest_first(time_count):
            block = segment_rows if shift == 0 else shifted(
                segment_rows, ("tm",), (time_count,), (shift,)
            )
            block_stats.append(group_stats(block, group_size, (0, 1, 2, 4)))
            source_time = (time_place - shift) % time_count
            clip = lax.dynamic_update_slice(clip, block, (source_time * frames, 0, 0, 0))
        while len(block_stats) > 1 and len(block_stats) % 2 == 0:
            block_stats = [
                merged_stats(block_stats[i], block_stats[i + 1])
                for i in range(0, len(block_stats), 2)
            ]
        stats1 = block_stats[0] if len(block_stats) == 1 else None
    else:
        copies = jnp.broadcast_to(latent[None], (row_count * time_count,) + latent.shape)
        gathered = lax.all_to_all(copies, ("rows", "tm"), 0, 0, tiled=True).reshape(
            (row_count, time_count, frames, rows_here, columns, channels)
        )
        clip = jnp.transpose(gathered, (1, 2, 0, 3, 4, 5)).reshape(
            (time_count * frames, all_rows, columns, channels)
        )
        stats1 = None

    if stats1 is None:
        stats1 = group_stats(clip, group_size, (0, 1, 2, 4))
    mean1, var1 = stats1
    frame_index = jnp.clip(
        time_place * frames - 2 + jnp.arange(frames + 2), 0, time_count * frames - 1
    )
    segment = jnp.take(clip, frame_index, axis=0)
    activated = jax.nn.silu(
        apply_norm(segment, mean1, var1, group_size) * norm1_gain + norm1_bias
    ).astype(jnp.bfloat16)
    padded_halves = [
        edge_pad(edge_pad(half, 1, 1, 1), 2, 1, 1) for half in chan_halves(activated)
    ]

    block_rows = conv_weight.shape[0]
    start = row_place * block_rows
    first_tap = start // C
    offset = start % C
    span = max(
        (place * block_rows + block_rows - 1) // C - (place * block_rows) // C + 1
        for place in range(row_count)
    )
    out_channels = conv_weight.shape[1]
    placed = lax.dynamic_update_slice(
        jnp.zeros((span * C, out_channels), conv_weight.dtype), conv_weight, (offset, 0)
    ).reshape(span, chan_count, channels, out_channels)
    taps = (block_rows * row_count) // C
    partial = None
    for shift, half in enumerate(padded_halves):
        source = (chan_place - shift) % chan_count
        windows = []
        for step in range(span):
            tap = jnp.minimum(first_tap + step, taps - 1)
            windows.append(
                lax.dynamic_slice(
                    half,
                    (tap // 9, (tap // 3) % 3, tap % 3, 0),
                    (frames, all_rows, columns, channels),
                ).reshape(-1, channels)
            )
        patches = jnp.concatenate(windows, axis=1)
        block = lax.dynamic_index_in_dim(placed, source, axis=1, keepdims=False).reshape(
            span * channels, out_channels
        )
        term = jnp.dot(patches, block, preferred_element_type=jnp.float32)
        partial = term if partial is None else partial + term

    pieces = partial.reshape(frames, row_count, rows_here, columns, out_channels)
    if row_count <= PERMUTE_GROUP:
        convolved = lax.dynamic_index_in_dim(pieces, row_place, axis=1, keepdims=False)
        for shift in nearest_first(row_count):
            chunk = lax.dynamic_index_in_dim(
                pieces, (row_place + shift) % row_count, axis=1, keepdims=False
            )
            convolved = convolved + shifted(chunk, ("rows",), (row_count,), (shift,))
    else:
        convolved = jnp.sum(lax.all_to_all(pieces, "rows", 1, 1, tiled=True), axis=1)
    own_middle = (latent.astype(jnp.float32) + convolved + conv_bias).astype(jnp.bfloat16)

    if row_count <= PERMUTE_GROUP:
        middle = jnp.zeros((frames, all_rows, columns, out_channels), own_middle.dtype)
        for shift in [0] + nearest_first(row_count):
            block = own_middle if shift == 0 else shifted(
                own_middle, ("rows",), (row_count,), (shift,)
            )
            source_row = (row_place - shift) % row_count
            middle = lax.dynamic_update_slice(middle, block, (0, source_row * rows_here, 0, 0))
    else:
        middle = lax.all_to_all(
            jnp.tile(own_middle, (1, row_count, 1, 1)), "rows", 1, 1, tiled=True
        )
    mean2, var2 = group_stats(middle, group_size, (1, 2, 4))
    normed = (apply_norm(middle, mean2, var2, group_size) * norm2_gain + norm2_bias).astype(
        jnp.bfloat16
    )
    normed_halves = chan_halves(normed)

    tokens = all_rows * columns
    local_tokens = rows_here * columns
    own_rows = [
        lax.dynamic_slice_in_dim(half, row_place * rows_here, rows_here, axis=1).reshape(
            -1, channels
        )
        for half in normed_halves
    ]
    flat = [half.reshape(-1, channels) for half in normed_halves]
    queries = (
        (split_dot(own_rows, w_query, channels) + b_query)
        .astype(jnp.bfloat16)
        .reshape(frames, local_tokens, C)
    )
    keys = split_dot(flat, w_key, channels).astype(jnp.bfloat16).reshape(frames, tokens, C)
    values = (
        (split_dot(flat, w_value, channels) + b_value)
        .astype(jnp.bfloat16)
        .reshape(frames, tokens, C)
    )
    scores = jnp.einsum("fqc,fkc->fqk", queries, keys, preferred_element_type=jnp.float32) * (
        C ** (-0.5)
    )
    row_peak = jnp.max(scores, axis=2, keepdims=True)
    weights = jnp.exp(scores - row_peak)
    weight_sum = jnp.sum(weights, axis=2, keepdims=True)
    attended = (
        jnp.einsum(
            "fqk,fkc->fqc",
            weights.astype(jnp.bfloat16),
            values,
            preferred_element_type=jnp.float32,
        )
        / weight_sum
    ).astype(jnp.bfloat16)
    out_block = lax.dynamic_slice(w_out, (0, chan_place * out_channels), (C, out_channels))
    out_bias = lax.dynamic_slice(b_out, (chan_place * out_channels,), (out_channels,))
    branch = (
        (jnp.dot(attended.reshape(-1, C), out_block, preferred_element_type=jnp.float32) + out_bias)
        .astype(jnp.bfloat16)
        .reshape(frames, rows_here, columns, out_channels)
    )
    return (own_middle.astype(jnp.float32) + branch.astype(jnp.float32)).astype(jnp.bfloat16)


def solution(mesh):
    in_specs = (
        P(("clips", "tm"), "rows", None, "chan"),
        P("chan"),
        P("chan"),
        P("rows", "chan"),
        P("chan"),
        P("chan"),
        P("chan"),
        P(),
        P(),
        P(),
        P(),
        P(),
        P(),
        P(),
    )
    out_specs = P(("clips", "tm"), "rows", None, "chan")
    return jax.shard_map(local, mesh=mesh, in_specs=in_specs, out_specs=out_specs, check_vma=False)
```

```python
import jax
import jax.numpy as jnp
from jax import lax
from jax.sharding import PartitionSpec as P

C = 512
GROUPS = 32


EPSILON = 1e-06


def group_stats(values, group_size, axes):
    grouped = values.astype(jnp.float32).reshape(
        values.shape[:-1] + (values.shape[-1] // group_size, group_size)
    )
    group_mean = jnp.mean(grouped, axis=axes, keepdims=True)
    centered = grouped - group_mean
    group_var = jnp.mean(centered * centered, axis=axes, keepdims=True)
    return group_mean, group_var


def apply_norm(values, group_mean, group_var, group_size):
    grouped = values.astype(jnp.float32).reshape(
        values.shape[:-1] + (values.shape[-1] // group_size, group_size)
    )
    return ((grouped - group_mean) * lax.rsqrt(group_var + EPSILON)).reshape(values.shape)


def edge_pad(cells, dim, before, after):
    size = cells.shape[dim]
    parts = [lax.slice_in_dim(cells, 0, 1, axis=dim)] * before + [cells]
    parts += [lax.slice_in_dim(cells, size - 1, size, axis=dim)] * after
    return jnp.concatenate(parts, axis=dim)


PERMUTE_GROUP = 8


def shifted(cells, axes, sizes, offsets):
    pairs = []
    places = [()]
    for size in sizes:
        places = [place + (i,) for place in places for i in range(size)]
    for place in places:
        target = tuple((p + o) % n for p, o, n in zip(place, offsets, sizes))
        source_index = 0
        target_index = 0
        for p, q, n in zip(place, target, sizes):
            source_index = source_index * n + p
            target_index = target_index * n + q
        pairs.append((source_index, target_index))
    return lax.ppermute(cells, axes, pairs)


def nearest_first(count):
    order = []
    for step in range(1, count):
        for shift in (step, count - step):
            if 0 < shift < count and shift not in order:
                order.append(shift)
    return order


def chan_halves(cells):
    count = lax.axis_size("chan")
    return [cells] + [
        lax.ppermute(cells, "chan", [(i, (i + shift) % count) for i in range(count)])
        for shift in range(1, count)
    ]


def half_rows(weight, shift, width):
    count = lax.axis_size("chan")
    source = (lax.axis_index("chan") - shift) % count
    return lax.dynamic_slice_in_dim(weight, source * width, width, axis=0)


def split_dot(halves, weight, width):
    total = None
    for shift, half in enumerate(halves):
        term = jnp.dot(half, half_rows(weight, shift, width), preferred_element_type=jnp.float32)
        total = term if total is None else total + term
    return total


def local(
    latent,
    norm1_gain,
    norm1_bias,
    conv_weight,
    conv_bias,
    norm2_gain,
    norm2_bias,
    w_query,
    b_query,
    w_key,
    w_value,
    b_value,
    w_out,
    b_out,
):
    frames, rows_here, columns, channels = latent.shape
    group_size = C // GROUPS
    time_count = lax.axis_size("tm")
    row_count = lax.axis_size("rows")
    chan_count = lax.axis_size("chan")
    time_place = lax.axis_index("tm")
    row_place = lax.axis_index("rows")
    chan_place = lax.axis_index("chan")
    all_rows = rows_here * row_count

    if row_count * time_count <= PERMUTE_GROUP:
        segment_rows = jnp.zeros((frames, all_rows, columns, channels), latent.dtype)
        for shift in [0] + nearest_first(row_count):
            block = latent if shift == 0 else shifted(latent, ("rows",), (row_count,), (shift,))
            source_row = (row_place - shift) % row_count
            segment_rows = lax.dynamic_update_slice(
                segment_rows, block, (0, source_row * rows_here, 0, 0)
            )
        clip = jnp.zeros((time_count * frames, all_rows, columns, channels), latent.dtype)
        for shift in [0] + nearest_first(time_count):
            block = segment_rows if shift == 0 else shifted(
                segment_rows, ("tm",), (time_count,), (shift,)
            )
            source_time = (time_place - shift) % time_count
            clip = lax.dynamic_update_slice(clip, block, (source_time * frames, 0, 0, 0))
    else:
        copies = jnp.broadcast_to(latent[None], (row_count * time_count,) + latent.shape)
        gathered = lax.all_to_all(copies, ("rows", "tm"), 0, 0, tiled=True).reshape(
            (row_count, time_count, frames, rows_here, columns, channels)
        )
        clip = jnp.transpose(gathered, (1, 2, 0, 3, 4, 5)).reshape(
            (time_count * frames, all_rows, columns, channels)
        )

    mean1, var1 = group_stats(clip, group_size, (0, 1, 2, 4))
    frame_index = jnp.clip(
        time_place * frames - 2 + jnp.arange(frames + 2), 0, time_count * frames - 1
    )
    segment = jnp.take(clip, frame_index, axis=0)
    activated = jax.nn.silu(
        apply_norm(segment, mean1, var1, group_size) * norm1_gain + norm1_bias
    ).astype(jnp.bfloat16)
    padded_halves = [
        edge_pad(edge_pad(half, 1, 1, 1), 2, 1, 1) for half in chan_halves(activated)
    ]

    block_rows = conv_weight.shape[0]
    start = row_place * block_rows
    first_tap = start // C
    offset = start % C
    span = max(
        (place * block_rows + block_rows - 1) // C - (place * block_rows) // C + 1
        for place in range(row_count)
    )
    out_channels = conv_weight.shape[1]
    placed = lax.dynamic_update_slice(
        jnp.zeros((span * C, out_channels), conv_weight.dtype), conv_weight, (offset, 0)
    ).reshape(span, chan_count, channels, out_channels)
    taps = (block_rows * row_count) // C
    all_patches = []
    for half in padded_halves:
        windows = []
        for step in range(span):
            tap = jnp.minimum(first_tap + step, taps - 1)
            windows.append(
                lax.dynamic_slice(
                    half,
                    (tap // 9, (tap // 3) % 3, tap % 3, 0),
                    (frames, all_rows, columns, channels),
                ).reshape(-1, channels)
            )
        all_patches.append(jnp.concatenate(windows, axis=1))
    all_patches = lax.optimization_barrier(all_patches)
    partial = None
    for shift, patches in enumerate(all_patches):
        source = (chan_place - shift) % chan_count
        block = lax.dynamic_index_in_dim(placed, source, axis=1, keepdims=False).reshape(
            span * channels, out_channels
        )
        term = jnp.dot(patches, block, preferred_element_type=jnp.float32)
        partial = term if partial is None else partial + term

    pieces = partial.reshape(frames, row_count, rows_here, columns, out_channels)
    if row_count <= PERMUTE_GROUP:
        convolved = lax.dynamic_index_in_dim(pieces, row_place, axis=1, keepdims=False)
        for shift in nearest_first(row_count):
            chunk = lax.dynamic_index_in_dim(
                pieces, (row_place + shift) % row_count, axis=1, keepdims=False
            )
            convolved = convolved + shifted(chunk, ("rows",), (row_count,), (shift,))
    else:
        convolved = jnp.sum(lax.all_to_all(pieces, "rows", 1, 1, tiled=True), axis=1)
    own_middle = (latent.astype(jnp.float32) + convolved + conv_bias).astype(jnp.bfloat16)

    if row_count <= PERMUTE_GROUP:
        middle = jnp.zeros((frames, all_rows, columns, out_channels), own_middle.dtype)
        for shift in [0] + nearest_first(row_count):
            block = own_middle if shift == 0 else shifted(
                own_middle, ("rows",), (row_count,), (shift,)
            )
            source_row = (row_place - shift) % row_count
            middle = lax.dynamic_update_slice(middle, block, (0, source_row * rows_here, 0, 0))
    else:
        middle = lax.all_to_all(
            jnp.tile(own_middle, (1, row_count, 1, 1)), "rows", 1, 1, tiled=True
        )
    mean2, var2 = group_stats(middle, group_size, (1, 2, 4))
    normed = (apply_norm(middle, mean2, var2, group_size) * norm2_gain + norm2_bias).astype(
        jnp.bfloat16
    )
    normed_halves = chan_halves(normed)

    tokens = all_rows * columns
    local_tokens = rows_here * columns
    own_rows = [
        lax.dynamic_slice_in_dim(half, row_place * rows_here, rows_here, axis=1).reshape(
            -1, channels
        )
        for half in normed_halves
    ]
    flat = [half.reshape(-1, channels) for half in normed_halves]
    queries = (
        (split_dot(own_rows, w_query, channels) + b_query)
        .astype(jnp.bfloat16)
        .reshape(frames, local_tokens, C)
    )
    keys = split_dot(flat, w_key, channels).astype(jnp.bfloat16).reshape(frames, tokens, C)
    values = (
        (split_dot(flat, w_value, channels) + b_value)
        .astype(jnp.bfloat16)
        .reshape(frames, tokens, C)
    )
    scores = jnp.einsum("fqc,fkc->fqk", queries, keys, preferred_element_type=jnp.float32) * (
        C ** (-0.5)
    )
    row_peak = jnp.max(scores, axis=2, keepdims=True)
    weights = jnp.exp(scores - row_peak)
    weight_sum = jnp.sum(weights, axis=2, keepdims=True)
    attended = (
        jnp.einsum(
            "fqk,fkc->fqc",
            weights.astype(jnp.bfloat16),
            values,
            preferred_element_type=jnp.float32,
        )
        / weight_sum
    ).astype(jnp.bfloat16)
    out_block = lax.dynamic_slice(w_out, (0, chan_place * out_channels), (C, out_channels))
    out_bias = lax.dynamic_slice(b_out, (chan_place * out_channels,), (out_channels,))
    branch = (
        (jnp.dot(attended.reshape(-1, C), out_block, preferred_element_type=jnp.float32) + out_bias)
        .astype(jnp.bfloat16)
        .reshape(frames, rows_here, columns, out_channels)
    )
    return (own_middle.astype(jnp.float32) + branch.astype(jnp.float32)).astype(jnp.bfloat16)


def solution(mesh):
    in_specs = (
        P(("clips", "tm"), "rows", None, "chan"),
        P("chan"),
        P("chan"),
        P("rows", "chan"),
        P("chan"),
        P("chan"),
        P("chan"),
        P(),
        P(),
        P(),
        P(),
        P(),
        P(),
        P(),
    )
    out_specs = P(("clips", "tm"), "rows", None, "chan")
    return jax.shard_map(local, mesh=mesh, in_specs=in_specs, out_specs=out_specs, check_vma=False)
```

```python
import jax
import jax.numpy as jnp
from jax import lax
from jax.sharding import PartitionSpec as P

C = 512
GROUPS = 32


EPSILON = 1e-06


def group_stats(values, group_size, axes):
    grouped = values.astype(jnp.float32).reshape(
        values.shape[:-1] + (values.shape[-1] // group_size, group_size)
    )
    group_mean = jnp.mean(grouped, axis=axes, keepdims=True)
    centered = grouped - group_mean
    group_var = jnp.mean(centered * centered, axis=axes, keepdims=True)
    return group_mean, group_var


def merged_stats(first, second):
    (mean_a, var_a), (mean_b, var_b) = first, second
    delta = mean_b - mean_a
    return mean_a + 0.5 * delta, 0.5 * (var_a + var_b) + 0.25 * delta * delta


def apply_norm(values, group_mean, group_var, group_size):
    grouped = values.astype(jnp.float32).reshape(
        values.shape[:-1] + (values.shape[-1] // group_size, group_size)
    )
    return ((grouped - group_mean) * lax.rsqrt(group_var + EPSILON)).reshape(values.shape)


def edge_pad(cells, dim, before, after):
    size = cells.shape[dim]
    parts = [lax.slice_in_dim(cells, 0, 1, axis=dim)] * before + [cells]
    parts += [lax.slice_in_dim(cells, size - 1, size, axis=dim)] * after
    return jnp.concatenate(parts, axis=dim)


PERMUTE_GROUP = 8


def shifted(cells, axes, sizes, offsets):
    pairs = []
    places = [()]
    for size in sizes:
        places = [place + (i,) for place in places for i in range(size)]
    for place in places:
        target = tuple((p + o) % n for p, o, n in zip(place, offsets, sizes))
        source_index = 0
        target_index = 0
        for p, q, n in zip(place, target, sizes):
            source_index = source_index * n + p
            target_index = target_index * n + q
        pairs.append((source_index, target_index))
    return lax.ppermute(cells, axes, pairs)


def nearest_first(count):
    order = []
    for step in range(1, count):
        for shift in (step, count - step):
            if 0 < shift < count and shift not in order:
                order.append(shift)
    return order


def chan_halves(cells):
    count = lax.axis_size("chan")
    return [cells] + [
        lax.ppermute(cells, "chan", [(i, (i + shift) % count) for i in range(count)])
        for shift in range(1, count)
    ]


def half_rows(weight, shift, width):
    count = lax.axis_size("chan")
    source = (lax.axis_index("chan") - shift) % count
    return lax.dynamic_slice_in_dim(weight, source * width, width, axis=0)


def split_dot(halves, weight, width):
    total = None
    for shift, half in enumerate(halves):
        term = jnp.dot(half, half_rows(weight, shift, width), preferred_element_type=jnp.float32)
        total = term if total is None else total + term
    return total


def local(
    latent,
    norm1_gain,
    norm1_bias,
    conv_weight,
    conv_bias,
    norm2_gain,
    norm2_bias,
    w_query,
    b_query,
    w_key,
    w_value,
    b_value,
    w_out,
    b_out,
):
    frames, rows_here, columns, channels = latent.shape
    group_size = C // GROUPS
    time_count = lax.axis_size("tm")
    row_count = lax.axis_size("rows")
    chan_count = lax.axis_size("chan")
    time_place = lax.axis_index("tm")
    row_place = lax.axis_index("rows")
    chan_place = lax.axis_index("chan")
    all_rows = rows_here * row_count

    if row_count * time_count <= PERMUTE_GROUP:
        segment_rows = jnp.zeros((frames, all_rows, columns, channels), latent.dtype)
        for shift in [0] + nearest_first(row_count):
            block = latent if shift == 0 else shifted(latent, ("rows",), (row_count,), (shift,))
            source_row = (row_place - shift) % row_count
            segment_rows = lax.dynamic_update_slice(
                segment_rows, block, (0, source_row * rows_here, 0, 0)
            )
        stats1 = None
        if time_count == 2:
            earlier = lax.ppermute(segment_rows, "tm", [(0, 1)])
            own_stats = group_stats(segment_rows, group_size, (0, 1, 2, 4))
            later_stats = lax.ppermute(own_stats, "tm", [(1, 0)])
            earlier_stats = group_stats(earlier, group_size, (0, 1, 2, 4))
            other_stats = tuple(
                jnp.where(time_place == 0, late, early)
                for late, early in zip(later_stats, earlier_stats)
            )
            stats1 = merged_stats(own_stats, other_stats)
            first = jnp.where(time_place == 0, segment_rows, earlier)
            clip = jnp.concatenate([first, segment_rows], axis=0)
        else:
            clip = jnp.zeros((time_count * frames, all_rows, columns, channels), latent.dtype)
            for shift in [0] + nearest_first(time_count):
                block = segment_rows if shift == 0 else shifted(
                    segment_rows, ("tm",), (time_count,), (shift,)
                )
                source_time = (time_place - shift) % time_count
                clip = lax.dynamic_update_slice(clip, block, (source_time * frames, 0, 0, 0))
    else:
        copies = jnp.broadcast_to(latent[None], (row_count * time_count,) + latent.shape)
        gathered = lax.all_to_all(copies, ("rows", "tm"), 0, 0, tiled=True).reshape(
            (row_count, time_count, frames, rows_here, columns, channels)
        )
        clip = jnp.transpose(gathered, (1, 2, 0, 3, 4, 5)).reshape(
            (time_count * frames, all_rows, columns, channels)
        )
        stats1 = None

    if stats1 is None:
        stats1 = group_stats(clip, group_size, (0, 1, 2, 4))
    mean1, var1 = stats1
    frame_index = jnp.clip(
        time_place * frames - 2 + jnp.arange(frames + 2), 0, time_count * frames - 1
    )
    segment = jnp.take(clip, frame_index, axis=0)
    activated = jax.nn.silu(
        apply_norm(segment, mean1, var1, group_size) * norm1_gain + norm1_bias
    ).astype(jnp.bfloat16)
    padded_halves = [
        edge_pad(edge_pad(half, 1, 1, 1), 2, 1, 1) for half in chan_halves(activated)
    ]

    block_rows = conv_weight.shape[0]
    start = row_place * block_rows
    first_tap = start // C
    offset = start % C
    span = max(
        (place * block_rows + block_rows - 1) // C - (place * block_rows) // C + 1
        for place in range(row_count)
    )
    out_channels = conv_weight.shape[1]
    placed = lax.dynamic_update_slice(
        jnp.zeros((span * C, out_channels), conv_weight.dtype), conv_weight, (offset, 0)
    ).reshape(span, chan_count, channels, out_channels)
    taps = (block_rows * row_count) // C
    partial = None
    for shift, half in enumerate(padded_halves):
        source = (chan_place - shift) % chan_count
        windows = []
        for step in range(span):
            tap = jnp.minimum(first_tap + step, taps - 1)
            windows.append(
                lax.dynamic_slice(
                    half,
                    (tap // 9, (tap // 3) % 3, tap % 3, 0),
                    (frames, all_rows, columns, channels),
                ).reshape(-1, channels)
            )
        patches = jnp.concatenate(windows, axis=1)
        block = lax.dynamic_index_in_dim(placed, source, axis=1, keepdims=False).reshape(
            span * channels, out_channels
        )
        term = jnp.dot(patches, block, preferred_element_type=jnp.float32)
        partial = term if partial is None else partial + term

    pieces = partial.reshape(frames, row_count, rows_here, columns, out_channels)
    if row_count <= PERMUTE_GROUP:
        convolved = lax.dynamic_index_in_dim(pieces, row_place, axis=1, keepdims=False)
        for shift in nearest_first(row_count):
            chunk = lax.dynamic_index_in_dim(
                pieces, (row_place + shift) % row_count, axis=1, keepdims=False
            )
            convolved = convolved + shifted(chunk, ("rows",), (row_count,), (shift,))
    else:
        convolved = jnp.sum(lax.all_to_all(pieces, "rows", 1, 1, tiled=True), axis=1)
    own_middle = (latent.astype(jnp.float32) + convolved + conv_bias).astype(jnp.bfloat16)

    if row_count <= PERMUTE_GROUP:
        middle = jnp.zeros((frames, all_rows, columns, out_channels), own_middle.dtype)
        for shift in [0] + nearest_first(row_count):
            block = own_middle if shift == 0 else shifted(
                own_middle, ("rows",), (row_count,), (shift,)
            )
            source_row = (row_place - shift) % row_count
            middle = lax.dynamic_update_slice(middle, block, (0, source_row * rows_here, 0, 0))
    else:
        middle = lax.all_to_all(
            jnp.tile(own_middle, (1, row_count, 1, 1)), "rows", 1, 1, tiled=True
        )
    mean2, var2 = group_stats(middle, group_size, (1, 2, 4))
    normed = (apply_norm(middle, mean2, var2, group_size) * norm2_gain + norm2_bias).astype(
        jnp.bfloat16
    )
    normed_halves = chan_halves(normed)

    tokens = all_rows * columns
    local_tokens = rows_here * columns
    own_rows = [
        lax.dynamic_slice_in_dim(half, row_place * rows_here, rows_here, axis=1).reshape(
            -1, channels
        )
        for half in normed_halves
    ]
    flat = [half.reshape(-1, channels) for half in normed_halves]
    queries = (
        (split_dot(own_rows, w_query, channels) + b_query)
        .astype(jnp.bfloat16)
        .reshape(frames, local_tokens, C)
    )
    keys = split_dot(flat, w_key, channels).astype(jnp.bfloat16).reshape(frames, tokens, C)
    values = (
        (split_dot(flat, w_value, channels) + b_value)
        .astype(jnp.bfloat16)
        .reshape(frames, tokens, C)
    )
    scores = jnp.einsum("fqc,fkc->fqk", queries, keys, preferred_element_type=jnp.float32) * (
        C ** (-0.5)
    )
    row_peak = jnp.max(scores, axis=2, keepdims=True)
    weights = jnp.exp(scores - row_peak)
    weight_sum = jnp.sum(weights, axis=2, keepdims=True)
    attended = (
        jnp.einsum(
            "fqk,fkc->fqc",
            weights.astype(jnp.bfloat16),
            values,
            preferred_element_type=jnp.float32,
        )
        / weight_sum
    ).astype(jnp.bfloat16)
    out_block = lax.dynamic_slice(w_out, (0, chan_place * out_channels), (C, out_channels))
    out_bias = lax.dynamic_slice(b_out, (chan_place * out_channels,), (out_channels,))
    branch = (
        (jnp.dot(attended.reshape(-1, C), out_block, preferred_element_type=jnp.float32) + out_bias)
        .astype(jnp.bfloat16)
        .reshape(frames, rows_here, columns, out_channels)
    )
    return (own_middle.astype(jnp.float32) + branch.astype(jnp.float32)).astype(jnp.bfloat16)


def solution(mesh):
    in_specs = (
        P(("clips", "tm"), "rows", None, "chan"),
        P("chan"),
        P("chan"),
        P("rows", "chan"),
        P("chan"),
        P("chan"),
        P("chan"),
        P(),
        P(),
        P(),
        P(),
        P(),
        P(),
        P(),
    )
    out_specs = P(("clips", "tm"), "rows", None, "chan")
    return jax.shard_map(local, mesh=mesh, in_specs=in_specs, out_specs=out_specs, check_vma=False)
```

```python
import jax
import jax.numpy as jnp
from jax import lax
from jax.sharding import PartitionSpec as P

C = 512
GROUPS = 32


EPSILON = 1e-06


def group_stats(values, group_size, axes):
    grouped = values.astype(jnp.float32).reshape(
        values.shape[:-1] + (values.shape[-1] // group_size, group_size)
    )
    group_mean = jnp.mean(grouped, axis=axes, keepdims=True)
    centered = grouped - group_mean
    group_var = jnp.mean(centered * centered, axis=axes, keepdims=True)
    return group_mean, group_var


def apply_norm(values, group_mean, group_var, group_size):
    grouped = values.astype(jnp.float32).reshape(
        values.shape[:-1] + (values.shape[-1] // group_size, group_size)
    )
    return ((grouped - group_mean) * lax.rsqrt(group_var + EPSILON)).reshape(values.shape)


def edge_pad(cells, dim, before, after):
    size = cells.shape[dim]
    parts = [lax.slice_in_dim(cells, 0, 1, axis=dim)] * before + [cells]
    parts += [lax.slice_in_dim(cells, size - 1, size, axis=dim)] * after
    return jnp.concatenate(parts, axis=dim)


PERMUTE_GROUP = 8


def shifted(cells, axes, sizes, offsets):
    pairs = []
    places = [()]
    for size in sizes:
        places = [place + (i,) for place in places for i in range(size)]
    for place in places:
        target = tuple((p + o) % n for p, o, n in zip(place, offsets, sizes))
        source_index = 0
        target_index = 0
        for p, q, n in zip(place, target, sizes):
            source_index = source_index * n + p
            target_index = target_index * n + q
        pairs.append((source_index, target_index))
    return lax.ppermute(cells, axes, pairs)


def nearest_first(count):
    order = []
    for step in range(1, count):
        for shift in (step, count - step):
            if 0 < shift < count and shift not in order:
                order.append(shift)
    return order


def chan_halves(cells):
    count = lax.axis_size("chan")
    return [cells] + [
        lax.ppermute(cells, "chan", [(i, (i + shift) % count) for i in range(count)])
        for shift in range(1, count)
    ]


def half_rows(weight, shift, width):
    count = lax.axis_size("chan")
    source = (lax.axis_index("chan") - shift) % count
    return lax.dynamic_slice_in_dim(weight, source * width, width, axis=0)


def split_dot(halves, weight, width):
    total = None
    for shift, half in enumerate(halves):
        term = jnp.dot(half, half_rows(weight, shift, width), preferred_element_type=jnp.float32)
        total = term if total is None else total + term
    return total


def local(
    latent,
    norm1_gain,
    norm1_bias,
    conv_weight,
    conv_bias,
    norm2_gain,
    norm2_bias,
    w_query,
    b_query,
    w_key,
    w_value,
    b_value,
    w_out,
    b_out,
):
    frames, rows_here, columns, channels = latent.shape
    group_size = C // GROUPS
    time_count = lax.axis_size("tm")
    row_count = lax.axis_size("rows")
    chan_count = lax.axis_size("chan")
    time_place = lax.axis_index("tm")
    row_place = lax.axis_index("rows")
    chan_place = lax.axis_index("chan")
    all_rows = rows_here * row_count

    if row_count * time_count <= PERMUTE_GROUP:
        segment_rows = jnp.zeros((frames, all_rows, columns, channels), latent.dtype)
        for shift in [0] + nearest_first(row_count):
            block = latent if shift == 0 else shifted(latent, ("rows",), (row_count,), (shift,))
            source_row = (row_place - shift) % row_count
            segment_rows = lax.dynamic_update_slice(
                segment_rows, block, (0, source_row * rows_here, 0, 0)
            )
        clip = jnp.zeros((time_count * frames, all_rows, columns, channels), latent.dtype)
        for shift in [0] + nearest_first(time_count):
            block = segment_rows if shift == 0 else shifted(
                segment_rows, ("tm",), (time_count,), (shift,)
            )
            source_time = (time_place - shift) % time_count
            clip = lax.dynamic_update_slice(clip, block, (source_time * frames, 0, 0, 0))
    else:
        copies = jnp.broadcast_to(latent[None], (row_count * time_count,) + latent.shape)
        gathered = lax.all_to_all(copies, ("rows", "tm"), 0, 0, tiled=True).reshape(
            (row_count, time_count, frames, rows_here, columns, channels)
        )
        clip = jnp.transpose(gathered, (1, 2, 0, 3, 4, 5)).reshape(
            (time_count * frames, all_rows, columns, channels)
        )

    mean1, var1 = group_stats(clip, group_size, (0, 1, 2, 4))
    frame_index = jnp.clip(
        time_place * frames - 2 + jnp.arange(frames + 2), 0, time_count * frames - 1
    )
    segment = jnp.take(clip, frame_index, axis=0)
    activated = jax.nn.silu(
        apply_norm(segment, mean1, var1, group_size) * norm1_gain + norm1_bias
    ).astype(jnp.bfloat16)
    padded_halves = [
        edge_pad(edge_pad(half, 1, 1, 1), 2, 1, 1) for half in chan_halves(activated)
    ]

    block_rows = conv_weight.shape[0]
    start = row_place * block_rows
    first_tap = start // C
    offset = start % C
    span = max(
        (place * block_rows + block_rows - 1) // C - (place * block_rows) // C + 1
        for place in range(row_count)
    )
    out_channels = conv_weight.shape[1]
    placed = lax.dynamic_update_slice(
        jnp.zeros((span * C, out_channels), conv_weight.dtype), conv_weight, (offset, 0)
    ).reshape(span, chan_count, channels, out_channels)
    taps = (block_rows * row_count) // C
    partial = None
    for shift, half in enumerate(padded_halves):
        source = (chan_place - shift) % chan_count
        windows = []
        for step in range(span):
            tap = jnp.minimum(first_tap + step, taps - 1)
            windows.append(
                lax.dynamic_slice(
                    half,
                    (tap // 9, (tap // 3) % 3, tap % 3, 0),
                    (frames, all_rows, columns, channels),
                )
                .transpose(1, 0, 2, 3)
                .reshape(-1, channels)
            )
        patches = jnp.concatenate(windows, axis=1)
        block = lax.dynamic_index_in_dim(placed, source, axis=1, keepdims=False).reshape(
            span * channels, out_channels
        )
        term = jnp.dot(patches, block, preferred_element_type=jnp.float32)
        partial = term if partial is None else partial + term

    pieces = partial.reshape(row_count, rows_here, frames, columns, out_channels)
    if row_count <= PERMUTE_GROUP:
        convolved = lax.dynamic_index_in_dim(pieces, row_place, axis=0, keepdims=False)
        for shift in nearest_first(row_count):
            chunk = lax.dynamic_index_in_dim(
                pieces, (row_place + shift) % row_count, axis=0, keepdims=False
            )
            convolved = convolved + shifted(chunk, ("rows",), (row_count,), (shift,))
    else:
        convolved = jnp.sum(lax.all_to_all(pieces, "rows", 0, 0, tiled=True), axis=0)
    convolved = jnp.transpose(convolved, (1, 0, 2, 3))
    own_middle = (latent.astype(jnp.float32) + convolved + conv_bias).astype(jnp.bfloat16)

    if row_count <= PERMUTE_GROUP:
        middle = jnp.zeros((frames, all_rows, columns, out_channels), own_middle.dtype)
        for shift in [0] + nearest_first(row_count):
            block = own_middle if shift == 0 else shifted(
                own_middle, ("rows",), (row_count,), (shift,)
            )
            source_row = (row_place - shift) % row_count
            middle = lax.dynamic_update_slice(middle, block, (0, source_row * rows_here, 0, 0))
    else:
        middle = lax.all_to_all(
            jnp.tile(own_middle, (1, row_count, 1, 1)), "rows", 1, 1, tiled=True
        )
    mean2, var2 = group_stats(middle, group_size, (1, 2, 4))
    normed = (apply_norm(middle, mean2, var2, group_size) * norm2_gain + norm2_bias).astype(
        jnp.bfloat16
    )
    normed_halves = chan_halves(normed)

    tokens = all_rows * columns
    local_tokens = rows_here * columns
    own_rows = [
        lax.dynamic_slice_in_dim(half, row_place * rows_here, rows_here, axis=1).reshape(
            -1, channels
        )
        for half in normed_halves
    ]
    flat = [half.reshape(-1, channels) for half in normed_halves]
    queries = (
        (split_dot(own_rows, w_query, channels) + b_query)
        .astype(jnp.bfloat16)
        .reshape(frames, local_tokens, C)
    )
    keys = split_dot(flat, w_key, channels).astype(jnp.bfloat16).reshape(frames, tokens, C)
    values = (
        (split_dot(flat, w_value, channels) + b_value)
        .astype(jnp.bfloat16)
        .reshape(frames, tokens, C)
    )
    scores = jnp.einsum("fqc,fkc->fqk", queries, keys, preferred_element_type=jnp.float32) * (
        C ** (-0.5)
    )
    row_peak = jnp.max(scores, axis=2, keepdims=True)
    weights = jnp.exp(scores - row_peak)
    weight_sum = jnp.sum(weights, axis=2, keepdims=True)
    attended = (
        jnp.einsum(
            "fqk,fkc->fqc",
            weights.astype(jnp.bfloat16),
            values,
            preferred_element_type=jnp.float32,
        )
        / weight_sum
    ).astype(jnp.bfloat16)
    out_block = lax.dynamic_slice(w_out, (0, chan_place * out_channels), (C, out_channels))
    out_bias = lax.dynamic_slice(b_out, (chan_place * out_channels,), (out_channels,))
    branch = (
        (jnp.dot(attended.reshape(-1, C), out_block, preferred_element_type=jnp.float32) + out_bias)
        .astype(jnp.bfloat16)
        .reshape(frames, rows_here, columns, out_channels)
    )
    return (own_middle.astype(jnp.float32) + branch.astype(jnp.float32)).astype(jnp.bfloat16)


def solution(mesh):
    in_specs = (
        P(("clips", "tm"), "rows", None, "chan"),
        P("chan"),
        P("chan"),
        P("rows", "chan"),
        P("chan"),
        P("chan"),
        P("chan"),
        P(),
        P(),
        P(),
        P(),
        P(),
        P(),
        P(),
    )
    out_specs = P(("clips", "tm"), "rows", None, "chan")
    return jax.shard_map(local, mesh=mesh, in_specs=in_specs, out_specs=out_specs, check_vma=False)
```

```python
import jax
import jax.numpy as jnp
from jax import lax
from jax.sharding import PartitionSpec as P

C = 512
GROUPS = 32


EPSILON = 1e-06


def group_stats(values, group_size, axes):
    grouped = values.astype(jnp.float32).reshape(
        values.shape[:-1] + (values.shape[-1] // group_size, group_size)
    )
    group_mean = jnp.mean(grouped, axis=axes, keepdims=True)
    centered = grouped - group_mean
    group_var = jnp.mean(centered * centered, axis=axes, keepdims=True)
    return group_mean, group_var


def apply_norm(values, group_mean, group_var, group_size):
    grouped = values.astype(jnp.float32).reshape(
        values.shape[:-1] + (values.shape[-1] // group_size, group_size)
    )
    return ((grouped - group_mean) * lax.rsqrt(group_var + EPSILON)).reshape(values.shape)


def edge_pad(cells, dim, before, after):
    size = cells.shape[dim]
    parts = [lax.slice_in_dim(cells, 0, 1, axis=dim)] * before + [cells]
    parts += [lax.slice_in_dim(cells, size - 1, size, axis=dim)] * after
    return jnp.concatenate(parts, axis=dim)


PERMUTE_GROUP = 8


def shifted(cells, axes, sizes, offsets):
    pairs = []
    places = [()]
    for size in sizes:
        places = [place + (i,) for place in places for i in range(size)]
    for place in places:
        target = tuple((p + o) % n for p, o, n in zip(place, offsets, sizes))
        source_index = 0
        target_index = 0
        for p, q, n in zip(place, target, sizes):
            source_index = source_index * n + p
            target_index = target_index * n + q
        pairs.append((source_index, target_index))
    return lax.ppermute(cells, axes, pairs)


def nearest_first(count):
    order = []
    for step in range(1, count):
        for shift in (step, count - step):
            if 0 < shift < count and shift not in order:
                order.append(shift)
    return order


def chan_halves(cells):
    count = lax.axis_size("chan")
    return [cells] + [
        lax.ppermute(cells, "chan", [(i, (i + shift) % count) for i in range(count)])
        for shift in range(1, count)
    ]


def half_rows(weight, shift, width):
    count = lax.axis_size("chan")
    source = (lax.axis_index("chan") - shift) % count
    return lax.dynamic_slice_in_dim(weight, source * width, width, axis=0)


def split_dot(halves, weight, width):
    total = None
    for shift, half in enumerate(halves):
        term = jnp.dot(half, half_rows(weight, shift, width), preferred_element_type=jnp.float32)
        total = term if total is None else total + term
    return total


def local(
    latent,
    norm1_gain,
    norm1_bias,
    conv_weight,
    conv_bias,
    norm2_gain,
    norm2_bias,
    w_query,
    b_query,
    w_key,
    w_value,
    b_value,
    w_out,
    b_out,
):
    frames, rows_here, columns, channels = latent.shape
    group_size = C // GROUPS
    time_count = lax.axis_size("tm")
    row_count = lax.axis_size("rows")
    chan_count = lax.axis_size("chan")
    time_place = lax.axis_index("tm")
    row_place = lax.axis_index("rows")
    chan_place = lax.axis_index("chan")
    all_rows = rows_here * row_count

    if row_count * time_count <= PERMUTE_GROUP:
        segment_rows = jnp.zeros((frames, all_rows, columns, channels), latent.dtype)
        for shift in [0] + nearest_first(row_count):
            block = latent if shift == 0 else shifted(latent, ("rows",), (row_count,), (shift,))
            source_row = (row_place - shift) % row_count
            segment_rows = lax.dynamic_update_slice(
                segment_rows, block, (0, source_row * rows_here, 0, 0)
            )
        clip = jnp.zeros((time_count * frames, all_rows, columns, channels), latent.dtype)
        for shift in [0] + nearest_first(time_count):
            block = segment_rows if shift == 0 else shifted(
                segment_rows, ("tm",), (time_count,), (shift,)
            )
            source_time = (time_place - shift) % time_count
            clip = lax.dynamic_update_slice(clip, block, (source_time * frames, 0, 0, 0))
    else:
        copies = jnp.broadcast_to(latent[None], (row_count * time_count,) + latent.shape)
        gathered = lax.all_to_all(copies, ("rows", "tm"), 0, 0, tiled=True).reshape(
            (row_count, time_count, frames, rows_here, columns, channels)
        )
        clip = jnp.transpose(gathered, (1, 2, 0, 3, 4, 5)).reshape(
            (time_count * frames, all_rows, columns, channels)
        )

    mean1, var1 = group_stats(clip, group_size, (0, 1, 2, 4))
    frame_index = jnp.clip(
        time_place * frames - 2 + jnp.arange(frames + 2), 0, time_count * frames - 1
    )
    segment = jnp.take(clip, frame_index, axis=0)
    activated = jax.nn.silu(
        apply_norm(segment, mean1, var1, group_size) * norm1_gain + norm1_bias
    ).astype(jnp.bfloat16)
    padded_halves = [
        edge_pad(edge_pad(half, 1, 1, 1), 2, 1, 1) for half in chan_halves(activated)
    ]

    block_rows = conv_weight.shape[0]
    start = row_place * block_rows
    first_tap = start // C
    offset = start % C
    span = max(
        (place * block_rows + block_rows - 1) // C - (place * block_rows) // C + 1
        for place in range(row_count)
    )
    out_channels = conv_weight.shape[1]
    placed = lax.dynamic_update_slice(
        jnp.zeros((span * C, out_channels), conv_weight.dtype), conv_weight, (offset, 0)
    ).reshape(span, chan_count, channels, out_channels)
    taps = (block_rows * row_count) // C
    partial = None
    for shift, half in enumerate(padded_halves):
        source = (chan_place - shift) % chan_count
        windows = []
        for step in range(span):
            tap = jnp.minimum(first_tap + step, taps - 1)
            windows.append(
                lax.dynamic_slice(
                    half,
                    (tap // 9, (tap // 3) % 3, tap % 3, 0),
                    (frames, all_rows, columns, channels),
                ).reshape(-1, channels)
            )
        patches = jnp.concatenate(windows, axis=1)
        block = lax.dynamic_index_in_dim(placed, source, axis=1, keepdims=False).reshape(
            span * channels, out_channels
        )
        term = jnp.dot(patches, block, preferred_element_type=jnp.float32)
        partial = term if partial is None else partial + term

    pieces = partial.reshape(frames, row_count, rows_here, columns, out_channels)
    if row_count <= PERMUTE_GROUP:
        convolved = lax.dynamic_index_in_dim(pieces, row_place, axis=1, keepdims=False)
        for shift in nearest_first(row_count)[::-1]:
            chunk = lax.dynamic_index_in_dim(
                pieces, (row_place + shift) % row_count, axis=1, keepdims=False
            )
            convolved = convolved + shifted(chunk, ("rows",), (row_count,), (shift,))
    else:
        convolved = jnp.sum(lax.all_to_all(pieces, "rows", 1, 1, tiled=True), axis=1)
    own_middle = (latent.astype(jnp.float32) + convolved + conv_bias).astype(jnp.bfloat16)

    if row_count <= PERMUTE_GROUP:
        middle = jnp.zeros((frames, all_rows, columns, out_channels), own_middle.dtype)
        for shift in [0] + nearest_first(row_count)[::-1]:
            block = own_middle if shift == 0 else shifted(
                own_middle, ("rows",), (row_count,), (shift,)
            )
            source_row = (row_place - shift) % row_count
            middle = lax.dynamic_update_slice(middle, block, (0, source_row * rows_here, 0, 0))
    else:
        middle = lax.all_to_all(
            jnp.tile(own_middle, (1, row_count, 1, 1)), "rows", 1, 1, tiled=True
        )
    mean2, var2 = group_stats(middle, group_size, (1, 2, 4))
    normed = (apply_norm(middle, mean2, var2, group_size) * norm2_gain + norm2_bias).astype(
        jnp.bfloat16
    )
    normed_halves = chan_halves(normed)

    tokens = all_rows * columns
    local_tokens = rows_here * columns
    own_rows = [
        lax.dynamic_slice_in_dim(half, row_place * rows_here, rows_here, axis=1).reshape(
            -1, channels
        )
        for half in normed_halves
    ]
    flat = [half.reshape(-1, channels) for half in normed_halves]
    queries = (
        (split_dot(own_rows, w_query, channels) + b_query)
        .astype(jnp.bfloat16)
        .reshape(frames, local_tokens, C)
    )
    keys = split_dot(flat, w_key, channels).astype(jnp.bfloat16).reshape(frames, tokens, C)
    values = (
        (split_dot(flat, w_value, channels) + b_value)
        .astype(jnp.bfloat16)
        .reshape(frames, tokens, C)
    )
    scores = jnp.einsum("fqc,fkc->fqk", queries, keys, preferred_element_type=jnp.float32) * (
        C ** (-0.5)
    )
    row_peak = jnp.max(scores, axis=2, keepdims=True)
    weights = jnp.exp(scores - row_peak)
    weight_sum = jnp.sum(weights, axis=2, keepdims=True)
    attended = (
        jnp.einsum(
            "fqk,fkc->fqc",
            weights.astype(jnp.bfloat16),
            values,
            preferred_element_type=jnp.float32,
        )
        / weight_sum
    ).astype(jnp.bfloat16)
    out_block = lax.dynamic_slice(w_out, (0, chan_place * out_channels), (C, out_channels))
    out_bias = lax.dynamic_slice(b_out, (chan_place * out_channels,), (out_channels,))
    branch = (
        (jnp.dot(attended.reshape(-1, C), out_block, preferred_element_type=jnp.float32) + out_bias)
        .astype(jnp.bfloat16)
        .reshape(frames, rows_here, columns, out_channels)
    )
    return (own_middle.astype(jnp.float32) + branch.astype(jnp.float32)).astype(jnp.bfloat16)


def solution(mesh):
    in_specs = (
        P(("clips", "tm"), "rows", None, "chan"),
        P("chan"),
        P("chan"),
        P("rows", "chan"),
        P("chan"),
        P("chan"),
        P("chan"),
        P(),
        P(),
        P(),
        P(),
        P(),
        P(),
        P(),
    )
    out_specs = P(("clips", "tm"), "rows", None, "chan")
    return jax.shard_map(local, mesh=mesh, in_specs=in_specs, out_specs=out_specs, check_vma=False)
```

```python
import jax
import jax.numpy as jnp
from jax import lax
from jax.sharding import PartitionSpec as P

C = 512
GROUPS = 32


EPSILON = 1e-06


def group_stats(values, group_size, axes):
    grouped = values.astype(jnp.float32).reshape(
        values.shape[:-1] + (values.shape[-1] // group_size, group_size)
    )
    group_mean = jnp.mean(grouped, axis=axes, keepdims=True)
    centered = grouped - group_mean
    group_var = jnp.mean(centered * centered, axis=axes, keepdims=True)
    return group_mean, group_var


def apply_norm(values, group_mean, group_var, group_size):
    grouped = values.astype(jnp.float32).reshape(
        values.shape[:-1] + (values.shape[-1] // group_size, group_size)
    )
    return ((grouped - group_mean) * lax.rsqrt(group_var + EPSILON)).reshape(values.shape)


def edge_pad(cells, dim, before, after):
    size = cells.shape[dim]
    parts = [lax.slice_in_dim(cells, 0, 1, axis=dim)] * before + [cells]
    parts += [lax.slice_in_dim(cells, size - 1, size, axis=dim)] * after
    return jnp.concatenate(parts, axis=dim)


PERMUTE_GROUP = 8


def shifted(cells, axes, sizes, offsets):
    pairs = []
    places = [()]
    for size in sizes:
        places = [place + (i,) for place in places for i in range(size)]
    for place in places:
        target = tuple((p + o) % n for p, o, n in zip(place, offsets, sizes))
        source_index = 0
        target_index = 0
        for p, q, n in zip(place, target, sizes):
            source_index = source_index * n + p
            target_index = target_index * n + q
        pairs.append((source_index, target_index))
    return lax.ppermute(cells, axes, pairs)


def nearest_first(count):
    order = []
    for step in range(1, count):
        for shift in (step, count - step):
            if 0 < shift < count and shift not in order:
                order.append(shift)
    return order


def chan_halves(cells):
    count = lax.axis_size("chan")
    return [cells] + [
        lax.ppermute(cells, "chan", [(i, (i + shift) % count) for i in range(count)])
        for shift in range(1, count)
    ]


def half_rows(weight, shift, width):
    count = lax.axis_size("chan")
    source = (lax.axis_index("chan") - shift) % count
    return lax.dynamic_slice_in_dim(weight, source * width, width, axis=0)


def split_dot(halves, weight, width):
    total = None
    for shift, half in enumerate(halves):
        term = jnp.dot(half, half_rows(weight, shift, width), preferred_element_type=jnp.float32)
        total = term if total is None else total + term
    return total


def local(
    latent,
    norm1_gain,
    norm1_bias,
    conv_weight,
    conv_bias,
    norm2_gain,
    norm2_bias,
    w_query,
    b_query,
    w_key,
    w_value,
    b_value,
    w_out,
    b_out,
):
    frames, rows_here, columns, channels = latent.shape
    group_size = C // GROUPS
    time_count = lax.axis_size("tm")
    row_count = lax.axis_size("rows")
    chan_count = lax.axis_size("chan")
    time_place = lax.axis_index("tm")
    row_place = lax.axis_index("rows")
    chan_place = lax.axis_index("chan")
    all_rows = rows_here * row_count

    if row_count * time_count <= PERMUTE_GROUP:
        segment_rows = jnp.zeros((frames, all_rows, columns, channels), latent.dtype)
        for shift in [0] + nearest_first(row_count):
            block = latent if shift == 0 else shifted(latent, ("rows",), (row_count,), (shift,))
            source_row = (row_place - shift) % row_count
            segment_rows = lax.dynamic_update_slice(
                segment_rows, block, (0, source_row * rows_here, 0, 0)
            )
        clip = jnp.zeros((time_count * frames, all_rows, columns, channels), latent.dtype)
        for shift in [0] + nearest_first(time_count):
            block = segment_rows if shift == 0 else shifted(
                segment_rows, ("tm",), (time_count,), (shift,)
            )
            source_time = (time_place - shift) % time_count
            clip = lax.dynamic_update_slice(clip, block, (source_time * frames, 0, 0, 0))
    else:
        copies = jnp.broadcast_to(latent[None], (row_count * time_count,) + latent.shape)
        gathered = lax.all_to_all(copies, ("rows", "tm"), 0, 0, tiled=True).reshape(
            (row_count, time_count, frames, rows_here, columns, channels)
        )
        clip = jnp.transpose(gathered, (1, 2, 0, 3, 4, 5)).reshape(
            (time_count * frames, all_rows, columns, channels)
        )

    mean1, var1 = group_stats(clip, group_size, (0, 1, 2, 4))
    segment = lax.dynamic_slice_in_dim(edge_pad(clip, 0, 2, 0), time_place * frames, frames + 2)
    activated = jax.nn.silu(
        apply_norm(segment, mean1, var1, group_size) * norm1_gain + norm1_bias
    ).astype(jnp.bfloat16)
    padded_halves = [
        edge_pad(edge_pad(half, 1, 1, 1), 2, 1, 1) for half in chan_halves(activated)
    ]

    block_rows = conv_weight.shape[0]
    start = row_place * block_rows
    first_tap = start // C
    offset = start % C
    span = max(
        (place * block_rows + block_rows - 1) // C - (place * block_rows) // C + 1
        for place in range(row_count)
    )
    out_channels = conv_weight.shape[1]
    placed = lax.dynamic_update_slice(
        jnp.zeros((span * C, out_channels), conv_weight.dtype), conv_weight, (offset, 0)
    ).reshape(span, chan_count, channels, out_channels)
    taps = (block_rows * row_count) // C
    partial = None
    for shift, half in enumerate(padded_halves):
        source = (chan_place - shift) % chan_count
        windows = []
        for step in range(span):
            tap = jnp.minimum(first_tap + step, taps - 1)
            windows.append(
                lax.dynamic_slice(
                    half,
                    (tap // 9, (tap // 3) % 3, tap % 3, 0),
                    (frames, all_rows, columns, channels),
                ).reshape(-1, channels)
            )
        patches = jnp.concatenate(windows, axis=1)
        block = lax.dynamic_index_in_dim(placed, source, axis=1, keepdims=False).reshape(
            span * channels, out_channels
        )
        term = jnp.dot(patches, block, preferred_element_type=jnp.float32)
        partial = term if partial is None else partial + term

    pieces = partial.reshape(frames, row_count, rows_here, columns, out_channels)
    if row_count <= PERMUTE_GROUP:
        convolved = lax.dynamic_index_in_dim(pieces, row_place, axis=1, keepdims=False)
        for shift in nearest_first(row_count):
            chunk = lax.dynamic_index_in_dim(
                pieces, (row_place + shift) % row_count, axis=1, keepdims=False
            )
            convolved = convolved + shifted(chunk, ("rows",), (row_count,), (shift,))
    else:
        convolved = jnp.sum(lax.all_to_all(pieces, "rows", 1, 1, tiled=True), axis=1)
    own_middle = (latent.astype(jnp.float32) + convolved + conv_bias).astype(jnp.bfloat16)

    if row_count <= PERMUTE_GROUP:
        middle = jnp.zeros((frames, all_rows, columns, out_channels), own_middle.dtype)
        for shift in [0] + nearest_first(row_count):
            block = own_middle if shift == 0 else shifted(
                own_middle, ("rows",), (row_count,), (shift,)
            )
            source_row = (row_place - shift) % row_count
            middle = lax.dynamic_update_slice(middle, block, (0, source_row * rows_here, 0, 0))
    else:
        middle = lax.all_to_all(
            jnp.tile(own_middle, (1, row_count, 1, 1)), "rows", 1, 1, tiled=True
        )
    mean2, var2 = group_stats(middle, group_size, (1, 2, 4))
    normed = (apply_norm(middle, mean2, var2, group_size) * norm2_gain + norm2_bias).astype(
        jnp.bfloat16
    )
    normed_halves = chan_halves(normed)

    tokens = all_rows * columns
    local_tokens = rows_here * columns
    own_rows = [
        lax.dynamic_slice_in_dim(half, row_place * rows_here, rows_here, axis=1).reshape(
            -1, channels
        )
        for half in normed_halves
    ]
    flat = [half.reshape(-1, channels) for half in normed_halves]
    queries = (
        (split_dot(own_rows, w_query, channels) + b_query)
        .astype(jnp.bfloat16)
        .reshape(frames, local_tokens, C)
    )
    keys = split_dot(flat, w_key, channels).astype(jnp.bfloat16).reshape(frames, tokens, C)
    values = (
        (split_dot(flat, w_value, channels) + b_value)
        .astype(jnp.bfloat16)
        .reshape(frames, tokens, C)
    )
    scores = jnp.einsum("fqc,fkc->fqk", queries, keys, preferred_element_type=jnp.float32) * (
        C ** (-0.5)
    )
    row_peak = jnp.max(scores, axis=2, keepdims=True)
    weights = jnp.exp(scores - row_peak)
    weight_sum = jnp.sum(weights, axis=2, keepdims=True)
    attended = (
        jnp.einsum(
            "fqk,fkc->fqc",
            weights.astype(jnp.bfloat16),
            values,
            preferred_element_type=jnp.float32,
        )
        / weight_sum
    ).astype(jnp.bfloat16)
    out_block = lax.dynamic_slice(w_out, (0, chan_place * out_channels), (C, out_channels))
    out_bias = lax.dynamic_slice(b_out, (chan_place * out_channels,), (out_channels,))
    branch = (
        (jnp.dot(attended.reshape(-1, C), out_block, preferred_element_type=jnp.float32) + out_bias)
        .astype(jnp.bfloat16)
        .reshape(frames, rows_here, columns, out_channels)
    )
    return (own_middle.astype(jnp.float32) + branch.astype(jnp.float32)).astype(jnp.bfloat16)


def solution(mesh):
    in_specs = (
        P(("clips", "tm"), "rows", None, "chan"),
        P("chan"),
        P("chan"),
        P("rows", "chan"),
        P("chan"),
        P("chan"),
        P("chan"),
        P(),
        P(),
        P(),
        P(),
        P(),
        P(),
        P(),
    )
    out_specs = P(("clips", "tm"), "rows", None, "chan")
    return jax.shard_map(local, mesh=mesh, in_specs=in_specs, out_specs=out_specs, check_vma=False)
```

```python
import jax
import jax.numpy as jnp
from jax import lax
from jax.sharding import PartitionSpec as P

C = 512
GROUPS = 32


EPSILON = 1e-06


def group_stats(values, group_size, axes):
    grouped = values.astype(jnp.float32).reshape(
        values.shape[:-1] + (values.shape[-1] // group_size, group_size)
    )
    group_mean = jnp.mean(grouped, axis=axes, keepdims=True)
    centered = grouped - group_mean
    group_var = jnp.mean(centered * centered, axis=axes, keepdims=True)
    return group_mean, group_var


def apply_norm(values, group_mean, group_var, group_size):
    grouped = values.astype(jnp.float32).reshape(
        values.shape[:-1] + (values.shape[-1] // group_size, group_size)
    )
    return ((grouped - group_mean) * lax.rsqrt(group_var + EPSILON)).reshape(values.shape)


def edge_pad(cells, dim, before, after):
    size = cells.shape[dim]
    parts = [lax.slice_in_dim(cells, 0, 1, axis=dim)] * before + [cells]
    parts += [lax.slice_in_dim(cells, size - 1, size, axis=dim)] * after
    return jnp.concatenate(parts, axis=dim)


PERMUTE_GROUP = 8


def shifted(cells, axes, sizes, offsets):
    pairs = []
    places = [()]
    for size in sizes:
        places = [place + (i,) for place in places for i in range(size)]
    for place in places:
        target = tuple((p + o) % n for p, o, n in zip(place, offsets, sizes))
        source_index = 0
        target_index = 0
        for p, q, n in zip(place, target, sizes):
            source_index = source_index * n + p
            target_index = target_index * n + q
        pairs.append((source_index, target_index))
    return lax.ppermute(cells, axes, pairs)


def nearest_first(count):
    order = []
    for step in range(1, count):
        for shift in (step, count - step):
            if 0 < shift < count and shift not in order:
                order.append(shift)
    return order


def chan_halves(cells):
    count = lax.axis_size("chan")
    return [cells] + [
        lax.ppermute(cells, "chan", [(i, (i + shift) % count) for i in range(count)])
        for shift in range(1, count)
    ]


def half_rows(weight, shift, width):
    count = lax.axis_size("chan")
    source = (lax.axis_index("chan") - shift) % count
    return lax.dynamic_slice_in_dim(weight, source * width, width, axis=0)


def split_dot(halves, weight, width):
    total = None
    for shift, half in enumerate(halves):
        term = jnp.dot(half, half_rows(weight, shift, width), preferred_element_type=jnp.float32)
        total = term if total is None else total + term
    return total


def local(
    latent,
    norm1_gain,
    norm1_bias,
    conv_weight,
    conv_bias,
    norm2_gain,
    norm2_bias,
    w_query,
    b_query,
    w_key,
    w_value,
    b_value,
    w_out,
    b_out,
):
    frames, rows_here, columns, channels = latent.shape
    group_size = C // GROUPS
    time_count = lax.axis_size("tm")
    row_count = lax.axis_size("rows")
    chan_count = lax.axis_size("chan")
    time_place = lax.axis_index("tm")
    row_place = lax.axis_index("rows")
    chan_place = lax.axis_index("chan")
    all_rows = rows_here * row_count

    if row_count * time_count <= PERMUTE_GROUP:
        segment_rows = jnp.zeros((frames, all_rows, columns, channels), latent.dtype)
        for shift in [0] + nearest_first(row_count):
            block = latent if shift == 0 else shifted(latent, ("rows",), (row_count,), (shift,))
            source_row = (row_place - shift) % row_count
            segment_rows = lax.dynamic_update_slice(
                segment_rows, block, (0, source_row * rows_here, 0, 0)
            )
        clip = jnp.zeros((time_count * frames, all_rows, columns, channels), latent.dtype)
        for shift in [0] + nearest_first(time_count):
            block = segment_rows if shift == 0 else shifted(
                segment_rows, ("tm",), (time_count,), (shift,)
            )
            source_time = (time_place - shift) % time_count
            clip = lax.dynamic_update_slice(clip, block, (source_time * frames, 0, 0, 0))
    else:
        copies = jnp.broadcast_to(latent[None], (row_count * time_count,) + latent.shape)
        gathered = lax.all_to_all(copies, ("rows", "tm"), 0, 0, tiled=True).reshape(
            (row_count, time_count, frames, rows_here, columns, channels)
        )
        clip = jnp.transpose(gathered, (1, 2, 0, 3, 4, 5)).reshape(
            (time_count * frames, all_rows, columns, channels)
        )

    mean1, var1 = group_stats(clip, group_size, (0, 1, 2, 4))
    segment = lax.dynamic_slice_in_dim(edge_pad(clip, 0, 2, 0), time_place * frames, frames + 2)
    own_padded = jax.nn.silu(
        apply_norm(edge_pad(edge_pad(segment, 1, 1, 1), 2, 1, 1), mean1, var1, group_size)
        * norm1_gain
        + norm1_bias
    ).astype(jnp.bfloat16)
    activated = own_padded[:, 1:-1, 1:-1]
    padded_halves = [own_padded] + [
        edge_pad(edge_pad(half, 1, 1, 1), 2, 1, 1) for half in chan_halves(activated)[1:]
    ]

    block_rows = conv_weight.shape[0]
    start = row_place * block_rows
    first_tap = start // C
    offset = start % C
    span = max(
        (place * block_rows + block_rows - 1) // C - (place * block_rows) // C + 1
        for place in range(row_count)
    )
    out_channels = conv_weight.shape[1]
    placed = lax.dynamic_update_slice(
        jnp.zeros((span * C, out_channels), conv_weight.dtype), conv_weight, (offset, 0)
    ).reshape(span, chan_count, channels, out_channels)
    taps = (block_rows * row_count) // C
    partial = None
    for shift, half in enumerate(padded_halves):
        source = (chan_place - shift) % chan_count
        windows = []
        for step in range(span):
            tap = jnp.minimum(first_tap + step, taps - 1)
            windows.append(
                lax.dynamic_slice(
                    half,
                    (tap // 9, (tap // 3) % 3, tap % 3, 0),
                    (frames, all_rows, columns, channels),
                ).reshape(-1, channels)
            )
        patches = jnp.concatenate(windows, axis=1)
        block = lax.dynamic_index_in_dim(placed, source, axis=1, keepdims=False).reshape(
            span * channels, out_channels
        )
        term = jnp.dot(patches, block, preferred_element_type=jnp.float32)
        partial = term if partial is None else partial + term

    pieces = partial.reshape(frames, row_count, rows_here, columns, out_channels)
    if row_count <= PERMUTE_GROUP:
        convolved = lax.dynamic_index_in_dim(pieces, row_place, axis=1, keepdims=False)
        for shift in nearest_first(row_count):
            chunk = lax.dynamic_index_in_dim(
                pieces, (row_place + shift) % row_count, axis=1, keepdims=False
            )
            convolved = convolved + shifted(chunk, ("rows",), (row_count,), (shift,))
    else:
        convolved = jnp.sum(lax.all_to_all(pieces, "rows", 1, 1, tiled=True), axis=1)
    own_middle = (latent.astype(jnp.float32) + convolved + conv_bias).astype(jnp.bfloat16)

    if row_count <= PERMUTE_GROUP:
        middle = jnp.zeros((frames, all_rows, columns, out_channels), own_middle.dtype)
        for shift in [0] + nearest_first(row_count):
            block = own_middle if shift == 0 else shifted(
                own_middle, ("rows",), (row_count,), (shift,)
            )
            source_row = (row_place - shift) % row_count
            middle = lax.dynamic_update_slice(middle, block, (0, source_row * rows_here, 0, 0))
    else:
        middle = lax.all_to_all(
            jnp.tile(own_middle, (1, row_count, 1, 1)), "rows", 1, 1, tiled=True
        )
    mean2, var2 = group_stats(middle, group_size, (1, 2, 4))
    normed = (apply_norm(middle, mean2, var2, group_size) * norm2_gain + norm2_bias).astype(
        jnp.bfloat16
    )
    normed_halves = chan_halves(normed)

    tokens = all_rows * columns
    local_tokens = rows_here * columns
    own_rows = [
        lax.dynamic_slice_in_dim(half, row_place * rows_here, rows_here, axis=1).reshape(
            -1, channels
        )
        for half in normed_halves
    ]
    flat = [half.reshape(-1, channels) for half in normed_halves]
    queries = (
        (split_dot(own_rows, w_query, channels) + b_query)
        .astype(jnp.bfloat16)
        .reshape(frames, local_tokens, C)
    )
    keys = split_dot(flat, w_key, channels).astype(jnp.bfloat16).reshape(frames, tokens, C)
    values = (
        (split_dot(flat, w_value, channels) + b_value)
        .astype(jnp.bfloat16)
        .reshape(frames, tokens, C)
    )
    scores = jnp.einsum("fqc,fkc->fqk", queries, keys, preferred_element_type=jnp.float32) * (
        C ** (-0.5)
    )
    row_peak = jnp.max(scores, axis=2, keepdims=True)
    weights = jnp.exp(scores - row_peak)
    weight_sum = jnp.sum(weights, axis=2, keepdims=True)
    attended = (
        jnp.einsum(
            "fqk,fkc->fqc",
            weights.astype(jnp.bfloat16),
            values,
            preferred_element_type=jnp.float32,
        )
        / weight_sum
    ).astype(jnp.bfloat16)
    out_block = lax.dynamic_slice(w_out, (0, chan_place * out_channels), (C, out_channels))
    out_bias = lax.dynamic_slice(b_out, (chan_place * out_channels,), (out_channels,))
    branch = (
        (jnp.dot(attended.reshape(-1, C), out_block, preferred_element_type=jnp.float32) + out_bias)
        .astype(jnp.bfloat16)
        .reshape(frames, rows_here, columns, out_channels)
    )
    return (own_middle.astype(jnp.float32) + branch.astype(jnp.float32)).astype(jnp.bfloat16)


def solution(mesh):
    in_specs = (
        P(("clips", "tm"), "rows", None, "chan"),
        P("chan"),
        P("chan"),
        P("rows", "chan"),
        P("chan"),
        P("chan"),
        P("chan"),
        P(),
        P(),
        P(),
        P(),
        P(),
        P(),
        P(),
    )
    out_specs = P(("clips", "tm"), "rows", None, "chan")
    return jax.shard_map(local, mesh=mesh, in_specs=in_specs, out_specs=out_specs, check_vma=False)
```

```python
import jax
import jax.numpy as jnp
from jax import lax
from jax.sharding import PartitionSpec as P

C = 512
GROUPS = 32


EPSILON = 1e-06


def group_stats(values, group_size, axes):
    grouped = values.astype(jnp.float32).reshape(
        values.shape[:-1] + (values.shape[-1] // group_size, group_size)
    )
    group_mean = jnp.mean(grouped, axis=axes, keepdims=True)
    centered = grouped - group_mean
    group_var = jnp.mean(centered * centered, axis=axes, keepdims=True)
    return group_mean, group_var


def apply_norm(values, group_mean, group_var, group_size):
    grouped = values.astype(jnp.float32).reshape(
        values.shape[:-1] + (values.shape[-1] // group_size, group_size)
    )
    return ((grouped - group_mean) * lax.rsqrt(group_var + EPSILON)).reshape(values.shape)


def edge_pad(cells, dim, before, after):
    size = cells.shape[dim]
    parts = [lax.slice_in_dim(cells, 0, 1, axis=dim)] * before + [cells]
    parts += [lax.slice_in_dim(cells, size - 1, size, axis=dim)] * after
    return jnp.concatenate(parts, axis=dim)


PERMUTE_GROUP = 8


def shifted(cells, axes, sizes, offsets):
    pairs = []
    places = [()]
    for size in sizes:
        places = [place + (i,) for place in places for i in range(size)]
    for place in places:
        target = tuple((p + o) % n for p, o, n in zip(place, offsets, sizes))
        source_index = 0
        target_index = 0
        for p, q, n in zip(place, target, sizes):
            source_index = source_index * n + p
            target_index = target_index * n + q
        pairs.append((source_index, target_index))
    return lax.ppermute(cells, axes, pairs)


def nearest_first(count):
    order = []
    for step in range(1, count):
        for shift in (step, count - step):
            if 0 < shift < count and shift not in order:
                order.append(shift)
    return order


def chan_halves(cells):
    count = lax.axis_size("chan")
    return [cells] + [
        lax.ppermute(cells, "chan", [(i, (i + shift) % count) for i in range(count)])
        for shift in range(1, count)
    ]


def half_rows(weight, shift, width):
    count = lax.axis_size("chan")
    source = (lax.axis_index("chan") - shift) % count
    return lax.dynamic_slice_in_dim(weight, source * width, width, axis=0)


def split_dot(halves, weight, width):
    total = None
    for shift, half in enumerate(halves):
        term = jnp.dot(half, half_rows(weight, shift, width), preferred_element_type=jnp.float32)
        total = term if total is None else total + term
    return total


def local(
    latent,
    norm1_gain,
    norm1_bias,
    conv_weight,
    conv_bias,
    norm2_gain,
    norm2_bias,
    w_query,
    b_query,
    w_key,
    w_value,
    b_value,
    w_out,
    b_out,
):
    frames, rows_here, columns, channels = latent.shape
    group_size = C // GROUPS
    time_count = lax.axis_size("tm")
    row_count = lax.axis_size("rows")
    chan_count = lax.axis_size("chan")
    time_place = lax.axis_index("tm")
    row_place = lax.axis_index("rows")
    chan_place = lax.axis_index("chan")
    all_rows = rows_here * row_count

    if row_count * time_count <= PERMUTE_GROUP:
        segment_rows = jnp.zeros((frames, all_rows, columns, channels), latent.dtype)
        for shift in [0] + nearest_first(row_count):
            block = latent if shift == 0 else shifted(latent, ("rows",), (row_count,), (shift,))
            source_row = (row_place - shift) % row_count
            segment_rows = lax.dynamic_update_slice(
                segment_rows, block, (0, source_row * rows_here, 0, 0)
            )
        clip = jnp.zeros((time_count * frames, all_rows, columns, channels), latent.dtype)
        for shift in [0] + nearest_first(time_count):
            block = segment_rows if shift == 0 else shifted(
                segment_rows, ("tm",), (time_count,), (shift,)
            )
            source_time = (time_place - shift) % time_count
            clip = lax.dynamic_update_slice(clip, block, (source_time * frames, 0, 0, 0))
    else:
        copies = jnp.broadcast_to(latent[None], (row_count * time_count,) + latent.shape)
        gathered = lax.all_to_all(copies, ("rows", "tm"), 0, 0, tiled=True).reshape(
            (row_count, time_count, frames, rows_here, columns, channels)
        )
        clip = jnp.transpose(gathered, (1, 2, 0, 3, 4, 5)).reshape(
            (time_count * frames, all_rows, columns, channels)
        )

    mean1, var1 = group_stats(clip, group_size, (0, 1, 2, 4))
    segment = lax.dynamic_slice_in_dim(edge_pad(clip, 0, 2, 0), time_place * frames, frames + 2)
    activated = jax.nn.silu(
        apply_norm(segment, mean1, var1, group_size) * norm1_gain + norm1_bias
    ).astype(jnp.bfloat16)
    padded_halves = [
        edge_pad(edge_pad(half, 1, 1, 1), 2, 1, 1) for half in chan_halves(activated)
    ]

    block_rows = conv_weight.shape[0]
    start = row_place * block_rows
    first_tap = start // C
    offset = start % C
    span = max(
        (place * block_rows + block_rows - 1) // C - (place * block_rows) // C + 1
        for place in range(row_count)
    )
    out_channels = conv_weight.shape[1]
    placed = lax.dynamic_update_slice(
        jnp.zeros((span * C, out_channels), conv_weight.dtype), conv_weight, (offset, 0)
    ).reshape(span, chan_count, channels, out_channels)
    taps = (block_rows * row_count) // C
    partial = None
    for shift, half in enumerate(padded_halves):
        source = (chan_place - shift) % chan_count
        windows = []
        for step in range(span):
            tap = jnp.minimum(first_tap + step, taps - 1)
            windows.append(
                lax.dynamic_slice(
                    half,
                    (tap // 9, (tap // 3) % 3, tap % 3, 0),
                    (frames, all_rows, columns, channels),
                ).reshape(-1, channels)
            )
        patches = jnp.concatenate(windows, axis=1)
        block = lax.dynamic_index_in_dim(placed, source, axis=1, keepdims=False).reshape(
            span * channels, out_channels
        )
        term = jnp.dot(patches, block, preferred_element_type=jnp.float32)
        partial = term if partial is None else partial + term

    pieces = partial.reshape(frames, row_count, rows_here, columns, out_channels)
    if row_count <= PERMUTE_GROUP:
        convolved = lax.dynamic_index_in_dim(pieces, row_place, axis=1, keepdims=False)
        for shift in nearest_first(row_count):
            chunk = lax.dynamic_index_in_dim(
                pieces, (row_place + shift) % row_count, axis=1, keepdims=False
            )
            convolved = convolved + shifted(chunk, ("rows",), (row_count,), (shift,))
    else:
        convolved = jnp.sum(lax.all_to_all(pieces, "rows", 1, 1, tiled=True), axis=1)
    own_middle = (latent.astype(jnp.float32) + convolved + conv_bias).astype(jnp.bfloat16)

    if row_count <= PERMUTE_GROUP:
        middle = jnp.concatenate(
            [own_middle]
            + [
                shifted(own_middle, ("rows",), (row_count,), (shift,))
                for shift in nearest_first(row_count)
            ],
            axis=1,
        )
        query_row = 0
    else:
        query_row = row_place * rows_here
        middle = lax.all_to_all(
            jnp.tile(own_middle, (1, row_count, 1, 1)), "rows", 1, 1, tiled=True
        )
    mean2, var2 = group_stats(middle, group_size, (1, 2, 4))
    normed = (apply_norm(middle, mean2, var2, group_size) * norm2_gain + norm2_bias).astype(
        jnp.bfloat16
    )
    normed_halves = chan_halves(normed)

    tokens = all_rows * columns
    local_tokens = rows_here * columns
    own_rows = [
        lax.dynamic_slice_in_dim(half, query_row, rows_here, axis=1).reshape(
            -1, channels
        )
        for half in normed_halves
    ]
    flat = [half.reshape(-1, channels) for half in normed_halves]
    queries = (
        (split_dot(own_rows, w_query, channels) + b_query)
        .astype(jnp.bfloat16)
        .reshape(frames, local_tokens, C)
    )
    keys = split_dot(flat, w_key, channels).astype(jnp.bfloat16).reshape(frames, tokens, C)
    values = (
        (split_dot(flat, w_value, channels) + b_value)
        .astype(jnp.bfloat16)
        .reshape(frames, tokens, C)
    )
    scores = jnp.einsum("fqc,fkc->fqk", queries, keys, preferred_element_type=jnp.float32) * (
        C ** (-0.5)
    )
    row_peak = jnp.max(scores, axis=2, keepdims=True)
    weights = jnp.exp(scores - row_peak)
    weight_sum = jnp.sum(weights, axis=2, keepdims=True)
    attended = (
        jnp.einsum(
            "fqk,fkc->fqc",
            weights.astype(jnp.bfloat16),
            values,
            preferred_element_type=jnp.float32,
        )
        / weight_sum
    ).astype(jnp.bfloat16)
    out_block = lax.dynamic_slice(w_out, (0, chan_place * out_channels), (C, out_channels))
    out_bias = lax.dynamic_slice(b_out, (chan_place * out_channels,), (out_channels,))
    branch = (
        (jnp.dot(attended.reshape(-1, C), out_block, preferred_element_type=jnp.float32) + out_bias)
        .astype(jnp.bfloat16)
        .reshape(frames, rows_here, columns, out_channels)
    )
    return (own_middle.astype(jnp.float32) + branch.astype(jnp.float32)).astype(jnp.bfloat16)


def solution(mesh):
    in_specs = (
        P(("clips", "tm"), "rows", None, "chan"),
        P("chan"),
        P("chan"),
        P("rows", "chan"),
        P("chan"),
        P("chan"),
        P("chan"),
        P(),
        P(),
        P(),
        P(),
        P(),
        P(),
        P(),
    )
    out_specs = P(("clips", "tm"), "rows", None, "chan")
    return jax.shard_map(local, mesh=mesh, in_specs=in_specs, out_specs=out_specs, check_vma=False)
```

```python
import jax
import jax.numpy as jnp
from jax import lax
from jax.sharding import PartitionSpec as P

C = 512
GROUPS = 32


EPSILON = 1e-06


def group_stats(values, group_size, axes):
    grouped = values.astype(jnp.float32).reshape(
        values.shape[:-1] + (values.shape[-1] // group_size, group_size)
    )
    group_mean = jnp.mean(grouped, axis=axes, keepdims=True)
    centered = grouped - group_mean
    group_var = jnp.mean(centered * centered, axis=axes, keepdims=True)
    return group_mean, group_var


def apply_norm(values, group_mean, group_var, group_size):
    grouped = values.astype(jnp.float32).reshape(
        values.shape[:-1] + (values.shape[-1] // group_size, group_size)
    )
    return ((grouped - group_mean) * lax.rsqrt(group_var + EPSILON)).reshape(values.shape)


def edge_pad(cells, dim, before, after):
    size = cells.shape[dim]
    parts = [lax.slice_in_dim(cells, 0, 1, axis=dim)] * before + [cells]
    parts += [lax.slice_in_dim(cells, size - 1, size, axis=dim)] * after
    return jnp.concatenate(parts, axis=dim)


PERMUTE_GROUP = 8


def shifted(cells, axes, sizes, offsets):
    pairs = []
    places = [()]
    for size in sizes:
        places = [place + (i,) for place in places for i in range(size)]
    for place in places:
        target = tuple((p + o) % n for p, o, n in zip(place, offsets, sizes))
        source_index = 0
        target_index = 0
        for p, q, n in zip(place, target, sizes):
            source_index = source_index * n + p
            target_index = target_index * n + q
        pairs.append((source_index, target_index))
    return lax.ppermute(cells, axes, pairs)


def nearest_first(count):
    order = []
    for step in range(1, count):
        for shift in (step, count - step):
            if 0 < shift < count and shift not in order:
                order.append(shift)
    return order


def chan_halves(cells):
    count = lax.axis_size("chan")
    return [cells] + [
        lax.ppermute(cells, "chan", [(i, (i + shift) % count) for i in range(count)])
        for shift in range(1, count)
    ]


def half_rows(weight, shift, width):
    count = lax.axis_size("chan")
    source = (lax.axis_index("chan") - shift) % count
    return lax.dynamic_slice_in_dim(weight, source * width, width, axis=0)


def split_dot(halves, weight, width):
    total = None
    for shift, half in enumerate(halves):
        term = jnp.dot(half, half_rows(weight, shift, width), preferred_element_type=jnp.float32)
        total = term if total is None else total + term
    return total


def local(
    latent,
    norm1_gain,
    norm1_bias,
    conv_weight,
    conv_bias,
    norm2_gain,
    norm2_bias,
    w_query,
    b_query,
    w_key,
    w_value,
    b_value,
    w_out,
    b_out,
):
    frames, rows_here, columns, channels = latent.shape
    group_size = C // GROUPS
    time_count = lax.axis_size("tm")
    row_count = lax.axis_size("rows")
    chan_count = lax.axis_size("chan")
    time_place = lax.axis_index("tm")
    row_place = lax.axis_index("rows")
    chan_place = lax.axis_index("chan")
    all_rows = rows_here * row_count

    if row_count * time_count <= PERMUTE_GROUP:
        segment_rows = jnp.zeros((frames, all_rows, columns, channels), latent.dtype)
        for shift in [0] + nearest_first(row_count):
            block = latent if shift == 0 else shifted(latent, ("rows",), (row_count,), (shift,))
            source_row = (row_place - shift) % row_count
            segment_rows = lax.dynamic_update_slice(
                segment_rows, block, (0, source_row * rows_here, 0, 0)
            )
        if time_count == 2:
            other = shifted(segment_rows, ("tm",), (2,), (1,))
            first = time_place == 0
            clip = jnp.concatenate(
                [jnp.where(first, segment_rows, other), jnp.where(first, other, segment_rows)],
                axis=0,
            )
        else:
            clip = jnp.zeros((time_count * frames, all_rows, columns, channels), latent.dtype)
            for shift in [0] + nearest_first(time_count):
                block = segment_rows if shift == 0 else shifted(
                    segment_rows, ("tm",), (time_count,), (shift,)
                )
                source_time = (time_place - shift) % time_count
                clip = lax.dynamic_update_slice(clip, block, (source_time * frames, 0, 0, 0))
    else:
        copies = jnp.broadcast_to(latent[None], (row_count * time_count,) + latent.shape)
        gathered = lax.all_to_all(copies, ("rows", "tm"), 0, 0, tiled=True).reshape(
            (row_count, time_count, frames, rows_here, columns, channels)
        )
        clip = jnp.transpose(gathered, (1, 2, 0, 3, 4, 5)).reshape(
            (time_count * frames, all_rows, columns, channels)
        )

    mean1, var1 = group_stats(clip, group_size, (0, 1, 2, 4))
    segment = lax.dynamic_slice_in_dim(edge_pad(clip, 0, 2, 0), time_place * frames, frames + 2)
    activated = jax.nn.silu(
        apply_norm(segment, mean1, var1, group_size) * norm1_gain + norm1_bias
    ).astype(jnp.bfloat16)
    padded_halves = [
        edge_pad(edge_pad(half, 1, 1, 1), 2, 1, 1) for half in chan_halves(activated)
    ]

    block_rows = conv_weight.shape[0]
    start = row_place * block_rows
    first_tap = start // C
    offset = start % C
    span = max(
        (place * block_rows + block_rows - 1) // C - (place * block_rows) // C + 1
        for place in range(row_count)
    )
    out_channels = conv_weight.shape[1]
    placed = lax.dynamic_update_slice(
        jnp.zeros((span * C, out_channels), conv_weight.dtype), conv_weight, (offset, 0)
    ).reshape(span, chan_count, channels, out_channels)
    taps = (block_rows * row_count) // C
    partial = None
    for shift, half in enumerate(padded_halves):
        source = (chan_place - shift) % chan_count
        windows = []
        for step in range(span):
            tap = jnp.minimum(first_tap + step, taps - 1)
            windows.append(
                lax.dynamic_slice(
                    half,
                    (tap // 9, (tap // 3) % 3, tap % 3, 0),
                    (frames, all_rows, columns, channels),
                ).reshape(-1, channels)
            )
        patches = jnp.concatenate(windows, axis=1)
        block = lax.dynamic_index_in_dim(placed, source, axis=1, keepdims=False).reshape(
            span * channels, out_channels
        )
        term = jnp.dot(patches, block, preferred_element_type=jnp.float32)
        partial = term if partial is None else partial + term

    pieces = partial.reshape(frames, row_count, rows_here, columns, out_channels)
    if row_count <= PERMUTE_GROUP:
        convolved = lax.dynamic_index_in_dim(pieces, row_place, axis=1, keepdims=False)
        for shift in nearest_first(row_count):
            chunk = lax.dynamic_index_in_dim(
                pieces, (row_place + shift) % row_count, axis=1, keepdims=False
            )
            convolved = convolved + shifted(chunk, ("rows",), (row_count,), (shift,))
    else:
        convolved = jnp.sum(lax.all_to_all(pieces, "rows", 1, 1, tiled=True), axis=1)
    own_middle = (latent.astype(jnp.float32) + convolved + conv_bias).astype(jnp.bfloat16)

    if row_count <= PERMUTE_GROUP:
        middle = jnp.zeros((frames, all_rows, columns, out_channels), own_middle.dtype)
        for shift in [0] + nearest_first(row_count):
            block = own_middle if shift == 0 else shifted(
                own_middle, ("rows",), (row_count,), (shift,)
            )
            source_row = (row_place - shift) % row_count
            middle = lax.dynamic_update_slice(middle, block, (0, source_row * rows_here, 0, 0))
    else:
        middle = lax.all_to_all(
            jnp.tile(own_middle, (1, row_count, 1, 1)), "rows", 1, 1, tiled=True
        )
    mean2, var2 = group_stats(middle, group_size, (1, 2, 4))
    normed = (apply_norm(middle, mean2, var2, group_size) * norm2_gain + norm2_bias).astype(
        jnp.bfloat16
    )
    normed_halves = chan_halves(normed)

    tokens = all_rows * columns
    local_tokens = rows_here * columns
    own_rows = [
        lax.dynamic_slice_in_dim(half, row_place * rows_here, rows_here, axis=1).reshape(
            -1, channels
        )
        for half in normed_halves
    ]
    flat = [half.reshape(-1, channels) for half in normed_halves]
    queries = (
        (split_dot(own_rows, w_query, channels) + b_query)
        .astype(jnp.bfloat16)
        .reshape(frames, local_tokens, C)
    )
    keys = split_dot(flat, w_key, channels).astype(jnp.bfloat16).reshape(frames, tokens, C)
    values = (
        (split_dot(flat, w_value, channels) + b_value)
        .astype(jnp.bfloat16)
        .reshape(frames, tokens, C)
    )
    scores = jnp.einsum("fqc,fkc->fqk", queries, keys, preferred_element_type=jnp.float32) * (
        C ** (-0.5)
    )
    row_peak = jnp.max(scores, axis=2, keepdims=True)
    weights = jnp.exp(scores - row_peak)
    weight_sum = jnp.sum(weights, axis=2, keepdims=True)
    attended = (
        jnp.einsum(
            "fqk,fkc->fqc",
            weights.astype(jnp.bfloat16),
            values,
            preferred_element_type=jnp.float32,
        )
        / weight_sum
    ).astype(jnp.bfloat16)
    out_block = lax.dynamic_slice(w_out, (0, chan_place * out_channels), (C, out_channels))
    out_bias = lax.dynamic_slice(b_out, (chan_place * out_channels,), (out_channels,))
    branch = (
        (jnp.dot(attended.reshape(-1, C), out_block, preferred_element_type=jnp.float32) + out_bias)
        .astype(jnp.bfloat16)
        .reshape(frames, rows_here, columns, out_channels)
    )
    return (own_middle.astype(jnp.float32) + branch.astype(jnp.float32)).astype(jnp.bfloat16)


def solution(mesh):
    in_specs = (
        P(("clips", "tm"), "rows", None, "chan"),
        P("chan"),
        P("chan"),
        P("rows", "chan"),
        P("chan"),
        P("chan"),
        P("chan"),
        P(),
        P(),
        P(),
        P(),
        P(),
        P(),
        P(),
    )
    out_specs = P(("clips", "tm"), "rows", None, "chan")
    return jax.shard_map(local, mesh=mesh, in_specs=in_specs, out_specs=out_specs, check_vma=False)
```
